32 devices in a mesh: ep: 16 (over z, y, x), tp: 2 (over core).
Axes of the slice: x: 2, y: 2, z: 4, core: 2. Of those that a mesh axis runs over, the one named last changes fastest.
Arguments:
- attn_heads: bfloat16 [2048, 2048], P('ep', 'tp'), may hold values from -6 to 6
- w_out: bfloat16 [2048, 2048], P('tp'), may hold values from -0.125 to 0.125
- resid_in: bfloat16 [2048, 2048], P('ep', 'tp'), may hold values from -6 to 6
- norm_gain: bfloat16 [2048], replicated, may hold values from 0.5 to 2
- router_w: bfloat16 [2048, 15], replicated, may hold values from -0.078125 to 0.078125
- expert_ids: int32 [2048, 4], P('ep'), may hold values from 0 to 14, all different within a row; in each aligned block of 128 rows (0 to 127, 128 to 255, ...) at most 51 rows name the same one
- copy_pick: int32 [2048, 4], P('ep'), may hold values 0 or 1
- slot_expert: int32 [16], replicated, may hold values from 0 to 14, as said below
- live_rows: int32 [16], P('ep'), may hold values from 1 to 128, as said below
- w_gate_up: bfloat16 [16, 2, 1408, 2048], P('ep', None, 'tp'), may hold values from -0.125 to 0.125
- w_down: bfloat16 [16, 1408, 2048], P('ep', 'tp'), may hold values from -0.3125 to 0.3125
Outputs:
- layer_out: bfloat16 [2048, 2048], P('ep', 'tp')
The draws below stay inside these ranges and needn't reach their ends.
Inputs may be any that keep to these rules, and one draw needn't show every extreme that they name: `expert_ids`: in each aligned block of 128 rows (the rows of one index of ep) no expert is named by more than 51 rows, a bound that some block reaches; the choices of a row are different experts. `copy_pick`: only matters where the chosen expert is held by two slots. `slot_expert`: every expert is held by one slot or two; exactly 1 expert are held by two. `live_rows`: some index of ep has all 128 rows live.
All inputs are finite; a program needn't handle non-finite values. No bound on the sum of `copy_pick` on one device may be relied on, other than what follows from the above.
Results may differ from the reference program's by a relative error of at most 0.017.
Values may be sent and summed in bfloat16 or wider, within the bound.
No kernel may reach another device: no remote copies, remote signals or barrier semaphores. Data moves between devices by JAX's collectives and lax.ppermute only.
A program may use at most 64 MiB of HBM per device.

```python
import math
import jax
import jax.numpy as jnp
import numpy as np
from jax import lax

D = 2048
FF = 1408
TOP = 4
TOK_DEV = 128
DUPLICATES = 1
EXPERTS = 15
CAP = 51
TOKENS = 2048
N_EP = 16
N_TP = 2


def draw_slot_expert(key, part):
    first_key, second_key = jax.random.split(jax.random.fold_in(key, 11))
    order = jax.random.permutation(first_key, EXPERTS + DUPLICATES)
    extra = jax.random.permutation(second_key, EXPERTS)[:DUPLICATES]
    listing = jnp.concatenate([jnp.arange(EXPERTS, dtype=jnp.int32), extra.astype(jnp.int32)])
    return jnp.zeros((EXPERTS + DUPLICATES,), jnp.int32).at[order].set(listing)


def draw_live_rows(key, part):
    first_key, second_key = jax.random.split(jax.random.fold_in(key, 23))
    counts = jax.random.randint(first_key, (N_EP,), TOK_DEV // 4 + 1, TOK_DEV + 1)
    fullest = jax.random.randint(second_key, (), 0, N_EP)
    return jnp.where(jnp.arange(N_EP) == fullest, TOK_DEV, counts).astype(jnp.int32)


def plant(values, key, smallest, high):
    longest = values.shape.index(max(values.shape))
    spots = []
    for shift in (0, 1):
        where = [jax.random.randint(jax.random.fold_in(key, axis), (), 0, length) for axis, length in enumerate(values.shape)]
        where[longest] = (where[longest] + shift) % values.shape[longest]
        spots.append(tuple(where))
    return values.at[spots[0]].set(smallest).at[spots[1]].set(high)


def levels(own_key, extent, pieces, least, largest):
    def one(axis_at, shards_of):
        heights = jax.random.uniform(jax.random.fold_in(jax.random.fold_in(own_key, 6), axis_at), (shards_of,), jnp.float32, least / len(pieces), largest / len(pieces))
        return jnp.repeat(jnp.exp(heights), extent[axis_at] // shards_of).reshape((-1,) + (1,) * (len(extent) - axis_at - 1))

    factor_of = one(*pieces[0])
    for cut in pieces[1:]:
        factor_of = factor_of * one(*cut)
    return factor_of


def deal_out(rng, own, number, rows, number_of, top, most, lean):
    sequence = jax.random.permutation(rng, number_of)
    heavy_load, common = portions_of(number_of, rows * top, most, lean, True), portions_of(number_of, rows * top, most, lean, False)
    places = jnp.arange(number_of)

    def named(tallies, rotation):
        used = int((tallies > 0).sum())
        fixed = max(1, used // 4)
        passed = fixed + (places - fixed + rotation * (used - fixed)) % max(1, number_of - fixed)
        return jnp.zeros((number_of,), jnp.int32).at[sequence[jnp.where(places < fixed, places, passed)]].set(jnp.asarray(tallies, jnp.int32))

    tallies = jnp.where(number % 4 == 0, named(heavy_load, number // 4), named(common, number - number // 4 - 1))
    mixed = jax.random.permutation(jax.random.fold_in(own, 3), number_of)
    source_of, receiver = mixed[0:number_of // 2 * 2:2], mixed[1:number_of // 2 * 2:2]
    margin = jnp.minimum(tallies[source_of] - 1, most - tallies[receiver]) // 2
    margin = jnp.where((source_of == sequence[0]) | (receiver == sequence[0]) | (tallies[receiver] == 0), 0, jnp.maximum(margin, 0))
    passed = jax.random.randint(jax.random.fold_in(own, 4), (number_of // 2,), 0, 1 << 20) % (margin + 1)
    tallies = tallies.at[source_of].add(-passed).at[receiver].add(passed)
    items = jnp.searchsorted(jnp.cumsum(tallies), jnp.arange(rows * top), side="right").astype(jnp.int32)
    table = items.reshape(top, rows).T
    table = table[jax.random.permutation(jax.random.fold_in(own, 1), rows)]
    rotation = jax.random.randint(jax.random.fold_in(own, 2), (rows, 1), 0, top)
    return jnp.take_along_axis(table, (jnp.arange(top)[None, :] + rotation) % top, axis=1)


def portions_of(number_of, total, most, skew, full):
    loads = [(1 << 20) // math.isqrt(grade ** skew) + 1 for grade in range(1, number_of + 1)]
    largest = most if full else min(most, max(-(-total // number_of), total * loads[0] // sum(loads)))
    least = 1 if total - largest >= number_of - 1 else 0
    holding, surplus = [largest] + [least] * (number_of - 1), total - largest - least * (number_of - 1)
    while surplus > 0:
        free = [i for i in range(1, number_of) if holding[i] < largest] or [i for i in range(1, number_of) if holding[i] < most]
        whole, budget = sum([loads[i] for i in free]), surplus
        for i in free:
            more = min(most - holding[i], max(1, budget * loads[i] // whole), surplus)
            holding[i] = holding[i] + more
            surplus = surplus - more
    return np.array(holding)


def gaussian(key, extent, scale, limit, cuts=(), kind=jnp.bfloat16):
    result = jax.random.normal(key, extent, jnp.float32) * scale
    if len(cuts) > 0:
        result = levels(key, extent, cuts, -0.22, 0.18) * result
    return jnp.clip(result, min=-limit, max=limit).astype(kind)


def setup_inputs(seed: int = 0) -> dict:
    key_of = jax.random.split(jax.random.key(seed), 12)
    attn_heads = gaussian(key_of[0], (TOKENS, D), 1.0, 6.0, ((0, 16), (1, 2)))
    w_out = gaussian(key_of[1], (D, D), D ** -0.5, 0.125, ((0, 2),))
    resid_in = gaussian(key_of[2], (TOKENS, D), 1.0, 6.0, ((0, 16), (1, 2)))
    norm_gain = jnp.clip(jnp.exp(jax.random.uniform(key_of[3], (D,), jnp.float32, math.log(0.5), math.log(2.0))), 0.5, 2.0).astype(jnp.bfloat16)
    router_w = gaussian(key_of[4], (D, EXPERTS), (3 * D) ** -0.5, 0.078125)
    expert_ids_keys = jax.random.split(jax.random.fold_in(key_of[5], 1), TOKENS // TOK_DEV)
    expert_ids_turns = jax.random.permutation(jax.random.fold_in(key_of[5], 3), TOKENS // TOK_DEV)
    expert_ids = jax.vmap(lambda own, number: deal_out(jax.random.fold_in(key_of[5], 2), own, number, TOK_DEV, EXPERTS, TOP, CAP, 2))(expert_ids_keys, expert_ids_turns).reshape((TOKENS, TOP))
    copy_pick = plant((jax.random.randint(key_of[6], (TOKENS, TOP), 0, 2) < 1).astype(jnp.int32), jax.random.fold_in(key_of[6], 1), 0, 1)
    slot_expert = draw_slot_expert(jax.random.fold_in(key_of[11], 71), 0)
    live_rows = draw_live_rows(jax.random.fold_in(key_of[11], 71), 0)
    w_gate_up = gaussian(key_of[9], (N_EP, 2, FF, D), D ** -0.5, 0.125, ((0, 16), (2, 2)))
    w_down = gaussian(key_of[10], (N_EP, FF, D), (FF // 4) ** -0.5, 0.3125, ((0, 16), (1, 2)))
    return {"attn_heads": attn_heads, "w_out": w_out, "resid_in": resid_in, "norm_gain": norm_gain, "router_w": router_w, "expert_ids": expert_ids, "copy_pick": copy_pick, "slot_expert": slot_expert, "live_rows": live_rows, "w_gate_up": w_gate_up, "w_down": w_down}


norm_eps = 1e-06

def destinations(expert_ids, copy_pick, slot_expert):
    slot_count = slot_expert.shape[0]
    slot_iota = jnp.arange(slot_count, dtype=jnp.int32)
    holders = expert_ids[:, :, None] == slot_expert[None, None, :]
    lower_slot = lax.optimization_barrier(jnp.min(jnp.where(holders, slot_iota, slot_count), axis=2))
    upper_slot = lax.optimization_barrier(jnp.max(jnp.where(holders, slot_iota, -1), axis=2))
    return jnp.where(copy_pick == 1, upper_slot, lower_slot).astype(jnp.int32)

def route_weights(normed, router_w, expert_ids):
    logits = jnp.dot(normed, router_w, preferred_element_type=jnp.float32)
    expert_iota = jnp.arange(router_w.shape[1], dtype=jnp.int32)
    chosen = lax.optimization_barrier(jnp.sum(jnp.where(expert_ids[:, :, None] == expert_iota, logits[:, None, :], 0.0), axis=2))
    powers = jnp.exp(chosen)
    return powers / lax.optimization_barrier(jnp.sum(powers, axis=1, keepdims=True))

def reference(attn_heads, w_out, resid_in, norm_gain, router_w, expert_ids, copy_pick, slot_expert, live_rows, w_gate_up, w_down):
    proj = jnp.dot(attn_heads, w_out, preferred_element_type=jnp.float32)
    stream = (resid_in.astype(jnp.float32) + proj).astype(jnp.bfloat16)
    stream_f = stream.astype(jnp.float32)
    scale = lax.rsqrt(lax.optimization_barrier(jnp.mean(stream_f * stream_f, axis=1, keepdims=True)) + norm_eps)
    normed = (stream_f * scale * norm_gain.astype(jnp.float32)).astype(jnp.bfloat16)
    weights = route_weights(normed, router_w, expert_ids)
    target = destinations(expert_ids, copy_pick, slot_expert)
    token_iota = jnp.arange(TOKENS, dtype=jnp.int32)
    alive = token_iota % TOK_DEV < live_rows[token_iota // TOK_DEV]
    pair_alive = jnp.broadcast_to(alive[:, None], target.shape)
    block_target = target.reshape(N_EP, TOK_DEV * TOP)
    block_alive = pair_alive.reshape(N_EP, TOK_DEV * TOP)
    slot_iota = jnp.arange(N_EP, dtype=jnp.int32)
    onehot = (block_target[:, :, None] == slot_iota) & block_alive[:, :, None]
    ranks = jnp.cumsum(onehot.astype(jnp.int32), axis=1) - 1
    position = lax.optimization_barrier(jnp.sum(jnp.where(onehot, ranks, 0), axis=2)).astype(jnp.int32)
    source = jnp.arange(N_EP, dtype=jnp.int32)[:, None]
    row_of = (source * CAP + position).reshape(-1).astype(jnp.int32)
    flat_target = target.reshape(-1)
    flat_alive = block_alive.reshape(-1)
    spread = jnp.repeat(normed, TOP, axis=0)
    slot_rows = N_EP * CAP

    def one_slot(slot):
        taken = flat_alive & (flat_target == slot)
        place = jnp.where(taken, row_of, slot_rows).astype(jnp.int32)
        inputs = jnp.zeros((slot_rows + 1, D), jnp.bfloat16).at[place].set(spread)[:slot_rows]
        pair = jnp.einsum('rd,gfd->rgf', inputs.astype(jnp.float32), w_gate_up[slot].astype(jnp.float32))
        hidden = (jax.nn.silu(pair[:, 0]) * pair[:, 1]).astype(jnp.bfloat16)
        groups = hidden.reshape(slot_rows, N_TP, FF // N_TP).astype(jnp.float32)
        down = w_down[slot].reshape(N_TP, FF // N_TP, D).astype(jnp.float32)
        shares = jnp.einsum('rjf,jfd->jrd', groups, down).astype(jnp.bfloat16)
        return lax.optimization_barrier(jnp.sum(shares.astype(jnp.float32), axis=0)).astype(jnp.bfloat16)
    results = lax.map(one_slot, slot_iota)
    fetched = results[flat_target, row_of].astype(jnp.float32).reshape(TOKENS, TOP, D)
    scaled = weights * alive[:, None].astype(jnp.float32)
    routed = lax.optimization_barrier(jnp.sum(fetched * scaled[:, :, None], axis=1))
    return (stream_f + routed).astype(jnp.bfloat16)
```

```python
import jax
import jax.numpy as jnp
from jax import lax
from jax.sharding import PartitionSpec as P

norm_eps = 1e-06


def destinations(expert_ids, copy_pick, slot_expert):
    slot_count = slot_expert.shape[0]
    slot_iota = jnp.arange(slot_count, dtype=jnp.int32)
    holders = expert_ids[:, :, None] == slot_expert[None, None, :]
    lower_slot = jnp.min(jnp.where(holders, slot_iota, slot_count), axis=2)
    upper_slot = jnp.max(jnp.where(holders, slot_iota, -1), axis=2)
    return jnp.where(copy_pick == 1, upper_slot, lower_slot)


def swap_tp(x):
    return lax.ppermute(x, "tp", perm=[(0, 1), (1, 0)])


def body(
    attn_heads,
    w_out,
    resid_in,
    norm_gain,
    router_w,
    expert_ids,
    copy_pick,
    slot_expert,
    live_rows,
    w_gate_up,
    w_down,
):
    tp_count = lax.axis_size("tp")
    ep_count = lax.axis_size("ep")
    tp_index = lax.axis_index("tp")
    tok_rows, slice_width = resid_in.shape
    full_width = slice_width * tp_count
    top_count = expert_ids.shape[1]
    bound = max(2, 3 * tok_rows * top_count // (2 * (ep_count - ep_count // 16)))
    capacity = -(-bound // 8) * 8
    slot_rows = ep_count * capacity
    offset = tp_index * slice_width
    pair_tp = tp_count == 2

    proj = jnp.dot(attn_heads, w_out, preferred_element_type=jnp.float32)
    resid_full = lax.dynamic_update_slice_in_dim(
        jnp.zeros((tok_rows, full_width), jnp.float32), resid_in.astype(jnp.float32), offset, 1
    )
    terms = proj + resid_full
    if pair_tp:
        total = terms + swap_tp(terms)
    else:
        total = lax.psum(terms, "tp")
    stream_full = total.astype(jnp.bfloat16).astype(jnp.float32)
    mean_sq = jnp.mean(stream_full * stream_full, axis=1, keepdims=True)
    scale = lax.rsqrt(mean_sq + norm_eps)
    normed_full = (stream_full * scale * norm_gain.astype(jnp.float32)).astype(jnp.bfloat16)
    normed_part = lax.dynamic_slice_in_dim(normed_full, offset, slice_width, 1)
    stream_part = lax.dynamic_slice_in_dim(stream_full, offset, slice_width, 1)

    logits = jnp.dot(normed_full, router_w, preferred_element_type=jnp.float32)
    expert_iota = jnp.arange(router_w.shape[1], dtype=jnp.int32)
    chosen = jnp.sum(
        jnp.where(expert_ids[:, :, None] == expert_iota, logits[:, None, :], 0.0), axis=2
    )
    powers = jnp.exp(chosen)
    weights = powers / jnp.sum(powers, axis=1, keepdims=True)
    target = destinations(expert_ids, copy_pick, slot_expert)
    alive = jnp.arange(tok_rows, dtype=jnp.int32) < live_rows[0]

    target_kt = target.T
    alive_kt = jnp.broadcast_to(alive[None, :], target_kt.shape)
    flat_target = target_kt.reshape(-1)
    flat_alive = alive_kt.reshape(-1)
    slot_iota = jnp.arange(ep_count, dtype=jnp.int32)
    onehot = (flat_target[:, None] == slot_iota[None, :]) & flat_alive[:, None]
    ranks = jnp.cumsum(onehot.astype(jnp.int32), axis=0) - 1
    position = jnp.sum(jnp.where(onehot, ranks, 0), axis=1)
    place = jnp.where(flat_alive, flat_target * capacity + position, -1)

    row_iota = jnp.arange(slot_rows, dtype=jnp.int32)
    pick = place[:, None] == row_iota[None, :]
    pick_kt = pick.reshape(top_count, tok_rows, slot_rows)
    spread = jnp.any(pick_kt, axis=0).astype(jnp.bfloat16)
    filled = lax.dot_general(
        spread, normed_part, (((0,), (0,)), ((), ())), preferred_element_type=jnp.float32
    ).astype(jnp.bfloat16)
    arrived = lax.all_to_all(
        filled.reshape(ep_count, capacity, slice_width),
        "ep",
        split_axis=0,
        concat_axis=0,
        tiled=True,
    ).reshape(slot_rows, slice_width)
    if pair_tp:
        other = swap_tp(arrived)
        first = jnp.where(tp_index == 0, arrived, other)
        second = jnp.where(tp_index == 0, other, arrived)
        inputs = jnp.concatenate([first, second], axis=1)
    else:
        inputs = lax.all_gather(arrived, "tp", axis=1, tiled=True)
    pair = jnp.einsum("rd,gfd->rgf", inputs, w_gate_up[0], preferred_element_type=jnp.float32)
    hidden = (jax.nn.silu(pair[:, 0]) * pair[:, 1]).astype(jnp.bfloat16)
    expert_terms = jnp.dot(hidden, w_down[0], preferred_element_type=jnp.float32).astype(
        jnp.bfloat16
    )
    if pair_tp:
        own = lax.dynamic_slice_in_dim(expert_terms, offset, slice_width, 1)
        away = lax.dynamic_slice_in_dim(expert_terms, slice_width - offset, slice_width, 1)
        results = (own.astype(jnp.float32) + swap_tp(away).astype(jnp.float32)).astype(
            jnp.bfloat16
        )
    else:
        results = lax.psum_scatter(expert_terms, "tp", scatter_dimension=1, tiled=True)
    returned = lax.all_to_all(
        results.reshape(ep_count, capacity, slice_width),
        "ep",
        split_axis=0,
        concat_axis=0,
        tiled=True,
    ).reshape(slot_rows, slice_width)

    fetched = jnp.dot(
        pick.astype(jnp.bfloat16), returned, preferred_element_type=jnp.float32
    ).reshape(top_count, tok_rows, slice_width)
    scaled = (weights * alive[:, None].astype(jnp.float32)).T
    routed = jnp.sum(fetched * scaled[:, :, None], axis=0)
    return (stream_part + routed).astype(jnp.bfloat16)


def solution(mesh):
    in_specs = (
        P("ep", "tp"),
        P("tp", None),
        P("ep", "tp"),
        P(),
        P(),
        P("ep", None),
        P("ep", None),
        P(),
        P("ep"),
        P("ep", None, "tp", None),
        P("ep", "tp", None),
    )
    out_specs = P("ep", "tp")
    return jax.shard_map(body, mesh=mesh, in_specs=in_specs, out_specs=out_specs, check_vma=False)
```

```python
import jax
import jax.numpy as jnp
from jax import lax
from jax.sharding import PartitionSpec as P

norm_eps = 1e-06


def destinations(expert_ids, copy_pick, slot_expert):
    slot_count = slot_expert.shape[0]
    slot_iota = jnp.arange(slot_count, dtype=jnp.int32)
    holders = expert_ids[:, :, None] == slot_expert[None, None, :]
    lower_slot = jnp.min(jnp.where(holders, slot_iota, slot_count), axis=2)
    upper_slot = jnp.max(jnp.where(holders, slot_iota, -1), axis=2)
    return jnp.where(copy_pick == 1, upper_slot, lower_slot)


def swap_tp(x):
    return lax.ppermute(x, "tp", perm=[(0, 1), (1, 0)])


def shift_exchange(blocks, sign):
    ep_count = blocks.shape[0]
    pieces = [blocks[0]]
    for k in range(1, ep_count):
        perm = [(i, (i + sign * k) % ep_count) for i in range(ep_count)]
        pieces.append(lax.ppermute(blocks[k], "ep", perm=perm))
    return jnp.stack(pieces, axis=0)


def body(
    attn_heads,
    w_out,
    resid_in,
    norm_gain,
    router_w,
    expert_ids,
    copy_pick,
    slot_expert,
    live_rows,
    w_gate_up,
    w_down,
):
    tp_count = lax.axis_size("tp")
    ep_count = lax.axis_size("ep")
    tp_index = lax.axis_index("tp")
    tok_rows, slice_width = resid_in.shape
    full_width = slice_width * tp_count
    top_count = expert_ids.shape[1]
    bound = max(2, 3 * tok_rows * top_count // (2 * (ep_count - ep_count // 16)))
    capacity = -(-bound // 8) * 8
    slot_rows = ep_count * capacity
    offset = tp_index * slice_width
    pair_tp = tp_count == 2

    proj = jnp.dot(attn_heads, w_out, preferred_element_type=jnp.float32)
    resid_full = lax.dynamic_update_slice_in_dim(
        jnp.zeros((tok_rows, full_width), jnp.float32), resid_in.astype(jnp.float32), offset, 1
    )
    terms = proj + resid_full
    if pair_tp:
        total = terms + swap_tp(terms)
    else:
        total = lax.psum(terms, "tp")
    stream_full = total.astype(jnp.bfloat16).astype(jnp.float32)
    mean_sq = jnp.mean(stream_full * stream_full, axis=1, keepdims=True)
    scale = lax.rsqrt(mean_sq + norm_eps)
    normed_full = (stream_full * scale * norm_gain.astype(jnp.float32)).astype(jnp.bfloat16)
    normed_part = lax.dynamic_slice_in_dim(normed_full, offset, slice_width, 1)
    stream_part = lax.dynamic_slice_in_dim(stream_full, offset, slice_width, 1)

    logits = jnp.dot(normed_full, router_w, preferred_element_type=jnp.float32)
    expert_iota = jnp.arange(router_w.shape[1], dtype=jnp.int32)
    chosen = jnp.sum(
        jnp.where(expert_ids[:, :, None] == expert_iota, logits[:, None, :], 0.0), axis=2
    )
    powers = jnp.exp(chosen)
    weights = powers / jnp.sum(powers, axis=1, keepdims=True)
    target = destinations(expert_ids, copy_pick, slot_expert)
    alive = jnp.arange(tok_rows, dtype=jnp.int32) < live_rows[0]

    target_kt = target.T
    alive_kt = jnp.broadcast_to(alive[None, :], target_kt.shape)
    flat_target = target_kt.reshape(-1)
    flat_alive = alive_kt.reshape(-1)
    slot_iota = jnp.arange(ep_count, dtype=jnp.int32)
    onehot = (flat_target[:, None] == slot_iota[None, :]) & flat_alive[:, None]
    ranks = jnp.cumsum(onehot.astype(jnp.int32), axis=0) - 1
    position = jnp.sum(jnp.where(onehot, ranks, 0), axis=1)
    ep_index = lax.axis_index("ep")
    shift = (flat_target - ep_index) % ep_count
    place = jnp.where(flat_alive, shift * capacity + position, -1)

    row_iota = jnp.arange(slot_rows, dtype=jnp.int32)
    pick = place[:, None] == row_iota[None, :]
    pick_kt = pick.reshape(top_count, tok_rows, slot_rows)
    spread = jnp.any(pick_kt, axis=0).astype(jnp.bfloat16)
    filled = lax.dot_general(
        spread, normed_part, (((0,), (0,)), ((), ())), preferred_element_type=jnp.float32
    ).astype(jnp.bfloat16)
    arrived = shift_exchange(filled.reshape(ep_count, capacity, slice_width), 1).reshape(
        slot_rows, slice_width
    )
    if pair_tp:
        other = swap_tp(arrived)
        first = jnp.where(tp_index == 0, arrived, other)
        second = jnp.where(tp_index == 0, other, arrived)
        inputs = jnp.concatenate([first, second], axis=1)
    else:
        inputs = lax.all_gather(arrived, "tp", axis=1, tiled=True)
    pair = jnp.einsum("rd,gfd->rgf", inputs, w_gate_up[0], preferred_element_type=jnp.float32)
    hidden = (jax.nn.silu(pair[:, 0]) * pair[:, 1]).astype(jnp.bfloat16)
    expert_terms = jnp.dot(hidden, w_down[0], preferred_element_type=jnp.float32).astype(
        jnp.bfloat16
    )
    if pair_tp:
        own = lax.dynamic_slice_in_dim(expert_terms, offset, slice_width, 1)
        away = lax.dynamic_slice_in_dim(expert_terms, slice_width - offset, slice_width, 1)
        results = (own.astype(jnp.float32) + swap_tp(away).astype(jnp.float32)).astype(
            jnp.bfloat16
        )
    else:
        results = lax.psum_scatter(expert_terms, "tp", scatter_dimension=1, tiled=True)
    returned = shift_exchange(results.reshape(ep_count, capacity, slice_width), -1).reshape(
        slot_rows, slice_width
    )

    fetched = jnp.dot(
        pick.astype(jnp.bfloat16), returned, preferred_element_type=jnp.float32
    ).reshape(top_count, tok_rows, slice_width)
    scaled = (weights * alive[:, None].astype(jnp.float32)).T
    routed = jnp.sum(fetched * scaled[:, :, None], axis=0)
    return (stream_part + routed).astype(jnp.bfloat16)


def solution(mesh):
    in_specs = (
        P("ep", "tp"),
        P("tp", None),
        P("ep", "tp"),
        P(),
        P(),
        P("ep", None),
        P("ep", None),
        P(),
        P("ep"),
        P("ep", None, "tp", None),
        P("ep", "tp", None),
    )
    out_specs = P("ep", "tp")
    return jax.shard_map(body, mesh=mesh, in_specs=in_specs, out_specs=out_specs, check_vma=False)
```

```python
import jax
import jax.numpy as jnp
from jax import lax
from jax.sharding import PartitionSpec as P

norm_eps = 1e-06


def destinations(expert_ids, copy_pick, slot_expert):
    slot_count = slot_expert.shape[0]
    slot_iota = jnp.arange(slot_count, dtype=jnp.int32)
    holders = expert_ids[:, :, None] == slot_expert[None, None, :]
    lower_slot = jnp.min(jnp.where(holders, slot_iota, slot_count), axis=2)
    upper_slot = jnp.max(jnp.where(holders, slot_iota, -1), axis=2)
    return jnp.where(copy_pick == 1, upper_slot, lower_slot)


def swap_tp(x):
    return lax.ppermute(x, "tp", perm=[(0, 1), (1, 0)])


def expert_chunk(place, normed_part, w_gate_up, w_down, ep_count, size, tp_index, pair_tp):
    tok_rows, slice_width = normed_part.shape
    top_count = place.shape[0] // tok_rows
    slot_rows = ep_count * size
    offset = tp_index * slice_width
    row_iota = jnp.arange(slot_rows, dtype=jnp.int32)
    pick = place[:, None] == row_iota[None, :]
    spread = jnp.any(pick.reshape(top_count, tok_rows, slot_rows), axis=0).astype(jnp.bfloat16)
    filled = lax.dot_general(
        spread, normed_part, (((0,), (0,)), ((), ())), preferred_element_type=jnp.float32
    ).astype(jnp.bfloat16)
    arrived = lax.all_to_all(
        filled.reshape(ep_count, size, slice_width),
        "ep",
        split_axis=0,
        concat_axis=0,
        tiled=True,
    ).reshape(slot_rows, slice_width)
    if pair_tp:
        other = swap_tp(arrived)
        first = jnp.where(tp_index == 0, arrived, other)
        second = jnp.where(tp_index == 0, other, arrived)
        inputs = jnp.concatenate([first, second], axis=1)
    else:
        inputs = lax.all_gather(arrived, "tp", axis=1, tiled=True)
    pair = jnp.einsum("rd,gfd->rgf", inputs, w_gate_up[0], preferred_element_type=jnp.float32)
    hidden = (jax.nn.silu(pair[:, 0]) * pair[:, 1]).astype(jnp.bfloat16)
    expert_terms = jnp.dot(hidden, w_down[0], preferred_element_type=jnp.float32).astype(
        jnp.bfloat16
    )
    if pair_tp:
        own = lax.dynamic_slice_in_dim(expert_terms, offset, slice_width, 1)
        away = lax.dynamic_slice_in_dim(expert_terms, slice_width - offset, slice_width, 1)
        results = (own.astype(jnp.float32) + swap_tp(away).astype(jnp.float32)).astype(
            jnp.bfloat16
        )
    else:
        results = lax.psum_scatter(expert_terms, "tp", scatter_dimension=1, tiled=True)
    returned = lax.all_to_all(
        results.reshape(ep_count, size, slice_width),
        "ep",
        split_axis=0,
        concat_axis=0,
        tiled=True,
    ).reshape(slot_rows, slice_width)
    return jnp.dot(pick.astype(jnp.bfloat16), returned, preferred_element_type=jnp.float32)


def body(
    attn_heads,
    w_out,
    resid_in,
    norm_gain,
    router_w,
    expert_ids,
    copy_pick,
    slot_expert,
    live_rows,
    w_gate_up,
    w_down,
):
    tp_count = lax.axis_size("tp")
    ep_count = lax.axis_size("ep")
    tp_index = lax.axis_index("tp")
    tok_rows, slice_width = resid_in.shape
    full_width = slice_width * tp_count
    top_count = expert_ids.shape[1]
    bound = max(2, 3 * tok_rows * top_count // (2 * (ep_count - ep_count // 16)))
    capacity = -(-bound // 8) * 8
    slot_rows = ep_count * capacity
    offset = tp_index * slice_width
    pair_tp = tp_count == 2

    proj = jnp.dot(attn_heads, w_out, preferred_element_type=jnp.float32)
    resid_full = lax.dynamic_update_slice_in_dim(
        jnp.zeros((tok_rows, full_width), jnp.float32), resid_in.astype(jnp.float32), offset, 1
    )
    terms = proj + resid_full
    if pair_tp:
        total = terms + swap_tp(terms)
    else:
        total = lax.psum(terms, "tp")
    stream_full = total.astype(jnp.bfloat16).astype(jnp.float32)
    mean_sq = jnp.mean(stream_full * stream_full, axis=1, keepdims=True)
    scale = lax.rsqrt(mean_sq + norm_eps)
    normed_full = (stream_full * scale * norm_gain.astype(jnp.float32)).astype(jnp.bfloat16)
    normed_part = lax.dynamic_slice_in_dim(normed_full, offset, slice_width, 1)
    stream_part = lax.dynamic_slice_in_dim(stream_full, offset, slice_width, 1)

    logits = jnp.dot(normed_full, router_w, preferred_element_type=jnp.float32)
    expert_iota = jnp.arange(router_w.shape[1], dtype=jnp.int32)
    chosen = jnp.sum(
        jnp.where(expert_ids[:, :, None] == expert_iota, logits[:, None, :], 0.0), axis=2
    )
    powers = jnp.exp(chosen)
    weights = powers / jnp.sum(powers, axis=1, keepdims=True)
    target = destinations(expert_ids, copy_pick, slot_expert)
    alive = jnp.arange(tok_rows, dtype=jnp.int32) < live_rows[0]

    target_kt = target.T
    alive_kt = jnp.broadcast_to(alive[None, :], target_kt.shape)
    flat_target = target_kt.reshape(-1)
    flat_alive = alive_kt.reshape(-1)
    slot_iota = jnp.arange(ep_count, dtype=jnp.int32)
    onehot = (flat_target[:, None] == slot_iota[None, :]) & flat_alive[:, None]
    ranks = jnp.cumsum(onehot.astype(jnp.int32), axis=0) - 1
    position = jnp.sum(jnp.where(onehot, ranks, 0), axis=1)

    head = max(8, capacity // 2 // 8 * 8)
    chunks = [(0, head), (head, capacity - head)] if capacity > head else [(0, capacity)]
    fetched = None
    for first_pos, size in chunks:
        inside = flat_alive & (position >= first_pos) & (position < first_pos + size)
        place = jnp.where(inside, flat_target * size + position - first_pos, -1)
        fetched_part = expert_chunk(
            place, normed_part, w_gate_up, w_down, ep_count, size, tp_index, pair_tp
        )
        fetched = fetched_part if fetched is None else fetched + fetched_part
    fetched = fetched.reshape(top_count, tok_rows, slice_width)
    scaled = (weights * alive[:, None].astype(jnp.float32)).T
    routed = jnp.sum(fetched * scaled[:, :, None], axis=0)
    return (stream_part + routed).astype(jnp.bfloat16)


def solution(mesh):
    in_specs = (
        P("ep", "tp"),
        P("tp", None),
        P("ep", "tp"),
        P(),
        P(),
        P("ep", None),
        P("ep", None),
        P(),
        P("ep"),
        P("ep", None, "tp", None),
        P("ep", "tp", None),
    )
    out_specs = P("ep", "tp")
    return jax.shard_map(body, mesh=mesh, in_specs=in_specs, out_specs=out_specs, check_vma=False)
```

```python
import jax
import jax.numpy as jnp
from jax import lax
from jax.sharding import PartitionSpec as P

norm_eps = 1e-06


def destinations(expert_ids, copy_pick, slot_expert):
    slot_count = slot_expert.shape[0]
    slot_iota = jnp.arange(slot_count, dtype=jnp.int32)
    holders = expert_ids[:, :, None] == slot_expert[None, None, :]
    lower_slot = jnp.min(jnp.where(holders, slot_iota, slot_count), axis=2)
    upper_slot = jnp.max(jnp.where(holders, slot_iota, -1), axis=2)
    return jnp.where(copy_pick == 1, upper_slot, lower_slot)


def swap_tp(x):
    return lax.ppermute(x, "tp", perm=[(0, 1), (1, 0)])


def body(
    attn_heads,
    w_out,
    resid_in,
    norm_gain,
    router_w,
    expert_ids,
    copy_pick,
    slot_expert,
    live_rows,
    w_gate_up,
    w_down,
):
    tp_count = lax.axis_size("tp")
    ep_count = lax.axis_size("ep")
    tp_index = lax.axis_index("tp")
    tok_rows, slice_width = resid_in.shape
    full_width = slice_width * tp_count
    top_count = expert_ids.shape[1]
    bound = max(2, 3 * tok_rows * top_count // (2 * (ep_count - ep_count // 16)))
    capacity = bound
    slot_rows = ep_count * capacity
    offset = tp_index * slice_width
    pair_tp = tp_count == 2

    proj = jnp.dot(attn_heads, w_out, preferred_element_type=jnp.float32)
    resid_full = lax.dynamic_update_slice_in_dim(
        jnp.zeros((tok_rows, full_width), jnp.float32), resid_in.astype(jnp.float32), offset, 1
    )
    terms = proj + resid_full
    if pair_tp:
        total = terms + swap_tp(terms)
    else:
        total = lax.psum(terms, "tp")
    stream_full = total.astype(jnp.bfloat16).astype(jnp.float32)
    mean_sq = jnp.mean(stream_full * stream_full, axis=1, keepdims=True)
    scale = lax.rsqrt(mean_sq + norm_eps)
    normed_full = (stream_full * scale * norm_gain.astype(jnp.float32)).astype(jnp.bfloat16)
    normed_part = lax.dynamic_slice_in_dim(normed_full, offset, slice_width, 1)
    stream_part = lax.dynamic_slice_in_dim(stream_full, offset, slice_width, 1)

    logits = jnp.dot(normed_full, router_w, preferred_element_type=jnp.float32)
    expert_iota = jnp.arange(router_w.shape[1], dtype=jnp.int32)
    chosen = jnp.sum(
        jnp.where(expert_ids[:, :, None] == expert_iota, logits[:, None, :], 0.0), axis=2
    )
    powers = jnp.exp(chosen)
    weights = powers / jnp.sum(powers, axis=1, keepdims=True)
    target = destinations(expert_ids, copy_pick, slot_expert)
    alive = jnp.arange(tok_rows, dtype=jnp.int32) < live_rows[0]

    target_kt = target.T
    alive_kt = jnp.broadcast_to(alive[None, :], target_kt.shape)
    flat_target = target_kt.reshape(-1)
    flat_alive = alive_kt.reshape(-1)
    slot_iota = jnp.arange(ep_count, dtype=jnp.int32)
    onehot = (flat_target[:, None] == slot_iota[None, :]) & flat_alive[:, None]
    ranks = jnp.cumsum(onehot.astype(jnp.int32), axis=0) - 1
    position = jnp.sum(jnp.where(onehot, ranks, 0), axis=1)
    place = jnp.where(flat_alive, flat_target * capacity + position, -1)

    row_iota = jnp.arange(slot_rows, dtype=jnp.int32)
    pick = place[:, None] == row_iota[None, :]
    pick_kt = pick.reshape(top_count, tok_rows, slot_rows)
    spread = jnp.any(pick_kt, axis=0).astype(jnp.bfloat16)
    filled = lax.dot_general(
        spread, normed_part, (((0,), (0,)), ((), ())), preferred_element_type=jnp.float32
    ).astype(jnp.bfloat16)
    arrived = lax.all_to_all(
        filled.reshape(ep_count, capacity, slice_width // 128, 128),
        "ep",
        split_axis=0,
        concat_axis=0,
        tiled=True,
    ).reshape(slot_rows, slice_width)
    if pair_tp:
        other = swap_tp(arrived)
        first = jnp.where(tp_index == 0, arrived, other)
        second = jnp.where(tp_index == 0, other, arrived)
        inputs = jnp.concatenate([first, second], axis=1)
    else:
        inputs = lax.all_gather(arrived, "tp", axis=1, tiled=True)
    pair = jnp.einsum("rd,gfd->rgf", inputs, w_gate_up[0], preferred_element_type=jnp.float32)
    hidden = (jax.nn.silu(pair[:, 0]) * pair[:, 1]).astype(jnp.bfloat16)
    expert_terms = jnp.dot(hidden, w_down[0], preferred_element_type=jnp.float32).astype(
        jnp.bfloat16
    )
    if pair_tp:
        own = lax.dynamic_slice_in_dim(expert_terms, offset, slice_width, 1)
        away = lax.dynamic_slice_in_dim(expert_terms, slice_width - offset, slice_width, 1)
        results = (own.astype(jnp.float32) + swap_tp(away).astype(jnp.float32)).astype(
            jnp.bfloat16
        )
    else:
        results = lax.psum_scatter(expert_terms, "tp", scatter_dimension=1, tiled=True)
    returned = lax.all_to_all(
        results.reshape(ep_count, capacity, slice_width // 128, 128),
        "ep",
        split_axis=0,
        concat_axis=0,
        tiled=True,
    ).reshape(slot_rows, slice_width)

    fetched = jnp.dot(
        pick.astype(jnp.bfloat16), returned, preferred_element_type=jnp.float32
    ).reshape(top_count, tok_rows, slice_width)
    scaled = (weights * alive[:, None].astype(jnp.float32)).T
    routed = jnp.sum(fetched * scaled[:, :, None], axis=0)
    return (stream_part + routed).astype(jnp.bfloat16)


def solution(mesh):
    in_specs = (
        P("ep", "tp"),
        P("tp", None),
        P("ep", "tp"),
        P(),
        P(),
        P("ep", None),
        P("ep", None),
        P(),
        P("ep"),
        P("ep", None, "tp", None),
        P("ep", "tp", None),
    )
    out_specs = P("ep", "tp")
    return jax.shard_map(body, mesh=mesh, in_specs=in_specs, out_specs=out_specs, check_vma=False)
```

```python
import jax
import jax.numpy as jnp
from jax import lax
from jax.sharding import PartitionSpec as P

norm_eps = 1e-06


def destinations(expert_ids, copy_pick, slot_expert):
    slot_count = slot_expert.shape[0]
    slot_iota = jnp.arange(slot_count, dtype=jnp.int32)
    holders = expert_ids[:, :, None] == slot_expert[None, None, :]
    lower_slot = jnp.min(jnp.where(holders, slot_iota, slot_count), axis=2)
    upper_slot = jnp.max(jnp.where(holders, slot_iota, -1), axis=2)
    return jnp.where(copy_pick == 1, upper_slot, lower_slot)


def swap_tp(x):
    return lax.ppermute(x, "tp", perm=[(0, 1), (1, 0)])


def body(
    attn_heads,
    w_out,
    resid_in,
    norm_gain,
    router_w,
    expert_ids,
    copy_pick,
    slot_expert,
    live_rows,
    w_gate_up,
    w_down,
):
    tp_count = lax.axis_size("tp")
    ep_count = lax.axis_size("ep")
    tp_index = lax.axis_index("tp")
    tok_rows, slice_width = resid_in.shape
    full_width = slice_width * tp_count
    top_count = expert_ids.shape[1]
    bound = max(2, 3 * tok_rows * top_count // (2 * (ep_count - ep_count // 16)))
    capacity = bound
    slot_rows = ep_count * capacity
    offset = tp_index * slice_width
    pair_tp = tp_count == 2

    proj = jnp.dot(attn_heads, w_out, preferred_element_type=jnp.float32)
    resid_full = lax.dynamic_update_slice_in_dim(
        jnp.zeros((tok_rows, full_width), jnp.float32), resid_in.astype(jnp.float32), offset, 1
    )
    terms = proj + resid_full
    if pair_tp:
        total = terms + swap_tp(terms)
    else:
        total = lax.psum(terms, "tp")
    stream_full = total.astype(jnp.bfloat16).astype(jnp.float32)
    mean_sq = jnp.mean(stream_full * stream_full, axis=1, keepdims=True)
    scale = lax.rsqrt(mean_sq + norm_eps)
    normed_full = (stream_full * scale * norm_gain.astype(jnp.float32)).astype(jnp.bfloat16)
    normed_part = lax.dynamic_slice_in_dim(normed_full, offset, slice_width, 1)
    stream_part = lax.dynamic_slice_in_dim(stream_full, offset, slice_width, 1)

    logits = jnp.dot(normed_full, router_w, preferred_element_type=jnp.float32)
    expert_iota = jnp.arange(router_w.shape[1], dtype=jnp.int32)
    chosen = jnp.sum(
        jnp.where(expert_ids[:, :, None] == expert_iota, logits[:, None, :], 0.0), axis=2
    )
    powers = jnp.exp(chosen)
    weights = powers / jnp.sum(powers, axis=1, keepdims=True)
    target = destinations(expert_ids, copy_pick, slot_expert)
    alive = jnp.arange(tok_rows, dtype=jnp.int32) < live_rows[0]

    target_kt = target.T
    alive_kt = jnp.broadcast_to(alive[None, :], target_kt.shape)
    flat_target = target_kt.reshape(-1)
    flat_alive = alive_kt.reshape(-1)
    slot_iota = jnp.arange(ep_count, dtype=jnp.int32)
    onehot = (flat_target[:, None] == slot_iota[None, :]) & flat_alive[:, None]
    ranks = jnp.cumsum(onehot.astype(jnp.int32), axis=0) - 1
    position = jnp.sum(jnp.where(onehot, ranks, 0), axis=1)
    place = jnp.where(flat_alive, flat_target * capacity + position, -1)

    row_iota = jnp.arange(slot_rows, dtype=jnp.int32)
    pick = place[:, None] == row_iota[None, :]
    pick_kt = pick.reshape(top_count, tok_rows, slot_rows)
    spread = jnp.any(pick_kt, axis=0).astype(jnp.bfloat16)
    filled = lax.dot_general(
        spread, normed_part, (((0,), (0,)), ((), ())), preferred_element_type=jnp.float32
    ).astype(jnp.bfloat16)
    arrived = lax.all_to_all(
        filled.reshape(ep_count, capacity, slice_width // 128, 128),
        "ep",
        split_axis=0,
        concat_axis=0,
        tiled=True,
    )
    if pair_tp:
        other = swap_tp(arrived)
        first = jnp.where(tp_index == 0, arrived, other).reshape(slot_rows, slice_width)
        second = jnp.where(tp_index == 0, other, arrived).reshape(slot_rows, slice_width)
        inputs = jnp.concatenate([first, second], axis=1)
    else:
        inputs = lax.all_gather(arrived.reshape(slot_rows, slice_width), "tp", axis=1, tiled=True)
    pair = jnp.einsum("rd,gfd->rgf", inputs, w_gate_up[0], preferred_element_type=jnp.float32)
    hidden = (jax.nn.silu(pair[:, 0]) * pair[:, 1]).astype(jnp.bfloat16)
    expert_terms = jnp.dot(hidden, w_down[0], preferred_element_type=jnp.float32).astype(
        jnp.bfloat16
    )
    if pair_tp:
        own = lax.dynamic_slice_in_dim(expert_terms, offset, slice_width, 1)
        away = lax.dynamic_slice_in_dim(expert_terms, slice_width - offset, slice_width, 1)
        results = (own.astype(jnp.float32) + swap_tp(away).astype(jnp.float32)).astype(
            jnp.bfloat16
        )
    else:
        results = lax.psum_scatter(expert_terms, "tp", scatter_dimension=1, tiled=True)
    returned = lax.all_to_all(
        results.reshape(ep_count, capacity, slice_width // 128, 128),
        "ep",
        split_axis=0,
        concat_axis=0,
        tiled=True,
    ).reshape(slot_rows, slice_width // 128, 128)

    fetched = lax.dot_general(
        pick.astype(jnp.bfloat16), returned, (((1,), (0,)), ((), ())),
        preferred_element_type=jnp.float32,
    ).reshape(top_count, tok_rows, slice_width)
    scaled = (weights * alive[:, None].astype(jnp.float32)).T
    routed = jnp.sum(fetched * scaled[:, :, None], axis=0)
    return (stream_part + routed).astype(jnp.bfloat16)


def solution(mesh):
    in_specs = (
        P("ep", "tp"),
        P("tp", None),
        P("ep", "tp"),
        P(),
        P(),
        P("ep", None),
        P("ep", None),
        P(),
        P("ep"),
        P("ep", None, "tp", None),
        P("ep", "tp", None),
    )
    out_specs = P("ep", "tp")
    return jax.shard_map(body, mesh=mesh, in_specs=in_specs, out_specs=out_specs, check_vma=False)
```

```python
import jax
import jax.numpy as jnp
from jax import lax
from jax.sharding import PartitionSpec as P

norm_eps = 1e-06


def destinations(expert_ids, copy_pick, slot_expert):
    slot_count = slot_expert.shape[0]
    slot_iota = jnp.arange(slot_count, dtype=jnp.int32)
    holders = expert_ids[:, :, None] == slot_expert[None, None, :]
    lower_slot = jnp.min(jnp.where(holders, slot_iota, slot_count), axis=2)
    upper_slot = jnp.max(jnp.where(holders, slot_iota, -1), axis=2)
    return jnp.where(copy_pick == 1, upper_slot, lower_slot)


def swap_tp(x):
    return lax.ppermute(x, "tp", perm=[(0, 1), (1, 0)])


def body(
    attn_heads,
    w_out,
    resid_in,
    norm_gain,
    router_w,
    expert_ids,
    copy_pick,
    slot_expert,
    live_rows,
    w_gate_up,
    w_down,
):
    tp_count = lax.axis_size("tp")
    ep_count = lax.axis_size("ep")
    tp_index = lax.axis_index("tp")
    tok_rows, slice_width = resid_in.shape
    full_width = slice_width * tp_count
    top_count = expert_ids.shape[1]
    bound = max(2, 3 * tok_rows * top_count // (2 * (ep_count - ep_count // 16)))
    capacity = bound
    slot_rows = ep_count * capacity
    offset = tp_index * slice_width
    pair_tp = tp_count == 2

    proj = jnp.dot(attn_heads, w_out, preferred_element_type=jnp.float32)
    resid_full = lax.dynamic_update_slice_in_dim(
        jnp.zeros((tok_rows, full_width), jnp.float32), resid_in.astype(jnp.float32), offset, 1
    )
    terms = proj + resid_full
    if pair_tp:
        total = terms + swap_tp(terms)
    else:
        total = lax.psum(terms, "tp")
    stream_full = total.astype(jnp.bfloat16).astype(jnp.float32)
    mean_sq = jnp.mean(stream_full * stream_full, axis=1, keepdims=True)
    scale = lax.rsqrt(mean_sq + norm_eps)
    normed_full = (stream_full * scale * norm_gain.astype(jnp.float32)).astype(jnp.bfloat16)
    normed_part = lax.dynamic_slice_in_dim(normed_full, offset, slice_width, 1)
    stream_part = lax.dynamic_slice_in_dim(stream_full, offset, slice_width, 1)

    logits = jnp.dot(normed_full, router_w, preferred_element_type=jnp.float32)
    expert_iota = jnp.arange(router_w.shape[1], dtype=jnp.int32)
    chosen = jnp.sum(
        jnp.where(expert_ids[:, :, None] == expert_iota, logits[:, None, :], 0.0), axis=2
    )
    powers = jnp.exp(chosen)
    weights = powers / jnp.sum(powers, axis=1, keepdims=True)
    target = destinations(expert_ids, copy_pick, slot_expert)
    alive = jnp.arange(tok_rows, dtype=jnp.int32) < live_rows[0]

    target_kt = target.T
    alive_kt = jnp.broadcast_to(alive[None, :], target_kt.shape)
    flat_target = target_kt.reshape(-1)
    flat_alive = alive_kt.reshape(-1)
    slot_iota = jnp.arange(ep_count, dtype=jnp.int32)
    onehot = (flat_target[:, None] == slot_iota[None, :]) & flat_alive[:, None]
    ranks = jnp.cumsum(onehot.astype(jnp.int32), axis=0) - 1
    position = jnp.sum(jnp.where(onehot, ranks, 0), axis=1)
    place = jnp.where(flat_alive, flat_target * capacity + position, -1)

    row_iota = jnp.arange(slot_rows, dtype=jnp.int32)
    pick = place[:, None] == row_iota[None, :]
    pick_kt = pick.reshape(top_count, tok_rows, slot_rows)
    spread = jnp.any(pick_kt, axis=0).astype(jnp.bfloat16)
    filled = lax.dot_general(
        spread, normed_part, (((0,), (0,)), ((), ())), preferred_element_type=jnp.float32
    ).astype(jnp.bfloat16)
    arrived = lax.all_to_all(
        filled.reshape(ep_count, capacity, slice_width // 128, 128),
        "ep",
        split_axis=0,
        concat_axis=0,
        tiled=True,
    )
    halves = 2 if ep_count % 2 == 0 else 1
    half_blocks = ep_count // halves
    half_rows = half_blocks * capacity
    result_parts = []
    for half in range(halves):
        block = arrived[half * half_blocks : (half + 1) * half_blocks]
        if pair_tp:
            other = swap_tp(block)
            first = jnp.where(tp_index == 0, block, other).reshape(half_rows, slice_width)
            second = jnp.where(tp_index == 0, other, block).reshape(half_rows, slice_width)
            inputs = jnp.concatenate([first, second], axis=1)
        else:
            inputs = lax.all_gather(block.reshape(half_rows, slice_width), "tp", axis=1, tiled=True)
        pair = jnp.einsum("rd,gfd->rgf", inputs, w_gate_up[0], preferred_element_type=jnp.float32)
        hidden = (jax.nn.silu(pair[:, 0]) * pair[:, 1]).astype(jnp.bfloat16)
        expert_terms = jnp.dot(hidden, w_down[0], preferred_element_type=jnp.float32).astype(
            jnp.bfloat16
        )
        if pair_tp:
            own = lax.dynamic_slice_in_dim(expert_terms, offset, slice_width, 1)
            away = lax.dynamic_slice_in_dim(expert_terms, slice_width - offset, slice_width, 1)
            part = (own.astype(jnp.float32) + swap_tp(away).astype(jnp.float32)).astype(
                jnp.bfloat16
            )
        else:
            part = lax.psum_scatter(expert_terms, "tp", scatter_dimension=1, tiled=True)
        result_parts.append(part.reshape(half_blocks, capacity, slice_width // 128, 128))
    results = jnp.concatenate(result_parts, axis=0)
    returned = lax.all_to_all(
        results,
        "ep",
        split_axis=0,
        concat_axis=0,
        tiled=True,
    ).reshape(slot_rows, slice_width // 128, 128)

    fetched = lax.dot_general(
        pick.astype(jnp.bfloat16), returned, (((1,), (0,)), ((), ())),
        preferred_element_type=jnp.float32,
    ).reshape(top_count, tok_rows, slice_width)
    scaled = (weights * alive[:, None].astype(jnp.float32)).T
    routed = jnp.sum(fetched * scaled[:, :, None], axis=0)
    return (stream_part + routed).astype(jnp.bfloat16)


def solution(mesh):
    in_specs = (
        P("ep", "tp"),
        P("tp", None),
        P("ep", "tp"),
        P(),
        P(),
        P("ep", None),
        P("ep", None),
        P(),
        P("ep"),
        P("ep", None, "tp", None),
        P("ep", "tp", None),
    )
    out_specs = P("ep", "tp")
    return jax.shard_map(body, mesh=mesh, in_specs=in_specs, out_specs=out_specs, check_vma=False)
```

```python
import jax
import jax.numpy as jnp
from jax import lax
from jax.sharding import PartitionSpec as P

norm_eps = 1e-06


def destinations(expert_ids, copy_pick, slot_expert):
    slot_count = slot_expert.shape[0]
    slot_iota = jnp.arange(slot_count, dtype=jnp.int32)
    holders = expert_ids[:, :, None] == slot_expert[None, None, :]
    lower_slot = jnp.min(jnp.where(holders, slot_iota, slot_count), axis=2)
    upper_slot = jnp.max(jnp.where(holders, slot_iota, -1), axis=2)
    return jnp.where(copy_pick == 1, upper_slot, lower_slot)


def swap_tp(x):
    return lax.ppermute(x, "tp", perm=[(0, 1), (1, 0)])


def body(
    attn_heads,
    w_out,
    resid_in,
    norm_gain,
    router_w,
    expert_ids,
    copy_pick,
    slot_expert,
    live_rows,
    w_gate_up,
    w_down,
):
    tp_count = lax.axis_size("tp")
    ep_count = lax.axis_size("ep")
    tp_index = lax.axis_index("tp")
    tok_rows, slice_width = resid_in.shape
    full_width = slice_width * tp_count
    top_count = expert_ids.shape[1]
    bound = max(2, 3 * tok_rows * top_count // (2 * (ep_count - ep_count // 16)))
    capacity = bound
    slot_rows = ep_count * capacity
    offset = tp_index * slice_width
    pair_tp = tp_count == 2

    proj = jnp.dot(attn_heads, w_out, preferred_element_type=jnp.float32)
    resid_full = lax.dynamic_update_slice_in_dim(
        jnp.zeros((tok_rows, full_width), jnp.float32), resid_in.astype(jnp.float32), offset, 1
    )
    terms = proj + resid_full
    if pair_tp:
        total = terms + swap_tp(terms)
    else:
        total = lax.psum(terms, "tp")
    stream_full = total.astype(jnp.bfloat16).astype(jnp.float32)
    mean_sq = jnp.mean(stream_full * stream_full, axis=1, keepdims=True)
    scale = lax.rsqrt(mean_sq + norm_eps)
    normed_full = (stream_full * scale * norm_gain.astype(jnp.float32)).astype(jnp.bfloat16)
    normed_part = lax.dynamic_slice_in_dim(normed_full, offset, slice_width, 1)
    stream_part = lax.dynamic_slice_in_dim(stream_full, offset, slice_width, 1)

    logits = jnp.dot(normed_full, router_w, preferred_element_type=jnp.float32)
    expert_iota = jnp.arange(router_w.shape[1], dtype=jnp.int32)
    chosen = jnp.sum(
        jnp.where(expert_ids[:, :, None] == expert_iota, logits[:, None, :], 0.0), axis=2
    )
    powers = jnp.exp(chosen)
    weights = powers / jnp.sum(powers, axis=1, keepdims=True)
    target = destinations(expert_ids, copy_pick, slot_expert)
    alive = jnp.arange(tok_rows, dtype=jnp.int32) < live_rows[0]

    target_kt = target.T
    alive_kt = jnp.broadcast_to(alive[None, :], target_kt.shape)
    flat_target = target_kt.reshape(-1)
    flat_alive = alive_kt.reshape(-1)
    slot_iota = jnp.arange(ep_count, dtype=jnp.int32)
    onehot = (flat_target[:, None] == slot_iota[None, :]) & flat_alive[:, None]
    ranks = jnp.cumsum(onehot.astype(jnp.int32), axis=0) - 1
    position = jnp.sum(jnp.where(onehot, ranks, 0), axis=1)
    place = jnp.where(flat_alive, flat_target * capacity + position, -1)

    row_iota = jnp.arange(slot_rows, dtype=jnp.int32)
    pick = place[:, None] == row_iota[None, :]
    pick_kt = pick.reshape(top_count, tok_rows, slot_rows)
    spread = jnp.any(pick_kt, axis=0).astype(jnp.bfloat16)
    filled = lax.dot_general(
        spread, normed_part, (((0,), (0,)), ((), ())), preferred_element_type=jnp.float32
    ).astype(jnp.bfloat16)
    arrived = lax.all_to_all(
        filled.reshape(ep_count, capacity, slice_width // 128, 128),
        "ep",
        split_axis=0,
        concat_axis=0,
        tiled=True,
    )
    if pair_tp:
        other = swap_tp(arrived)
        first = jnp.where(tp_index == 0, arrived, other).reshape(slot_rows, slice_width)
        second = jnp.where(tp_index == 0, other, arrived).reshape(slot_rows, slice_width)
        inputs = jnp.concatenate([first, second], axis=1)
    else:
        inputs = lax.all_gather(arrived.reshape(slot_rows, slice_width), "tp", axis=1, tiled=True)
    pair = jnp.einsum("rd,gfd->rgf", inputs, w_gate_up[0], preferred_element_type=jnp.float32)
    hidden = (jax.nn.silu(pair[:, 0]) * pair[:, 1]).astype(jnp.bfloat16)
    expert_terms = jnp.dot(hidden, w_down[0], preferred_element_type=jnp.float32).astype(
        jnp.bfloat16
    )
    if pair_tp:
        own = lax.dynamic_slice_in_dim(expert_terms, offset, slice_width, 1)
        away = lax.dynamic_slice_in_dim(expert_terms, slice_width - offset, slice_width, 1)
        results = (own.astype(jnp.float32) + swap_tp(away).astype(jnp.float32)).astype(
            jnp.bfloat16
        )
    else:
        results = lax.psum_scatter(expert_terms, "tp", scatter_dimension=1, tiled=True)
    returned = lax.all_to_all(
        results.reshape(ep_count, capacity, slice_width // 128, 128),
        "ep",
        split_axis=0,
        concat_axis=0,
        tiled=True,
    ).reshape(slot_rows, slice_width // 128, 128)

    fetched = jnp.take(returned, jnp.maximum(place, 0), axis=0, mode="clip").astype(jnp.float32)
    fetched = fetched.reshape(top_count, tok_rows, slice_width // 128, 128)
    scaled = (weights * alive[:, None].astype(jnp.float32)).T
    routed = jnp.sum(fetched * scaled[:, :, None, None], axis=0).reshape(tok_rows, slice_width)
    return (stream_part + routed).astype(jnp.bfloat16)


def solution(mesh):
    in_specs = (
        P("ep", "tp"),
        P("tp", None),
        P("ep", "tp"),
        P(),
        P(),
        P("ep", None),
        P("ep", None),
        P(),
        P("ep"),
        P("ep", None, "tp", None),
        P("ep", "tp", None),
    )
    out_specs = P("ep", "tp")
    return jax.shard_map(body, mesh=mesh, in_specs=in_specs, out_specs=out_specs, check_vma=False)
```

```python
import jax
import jax.numpy as jnp
from jax import lax
from jax.sharding import PartitionSpec as P

norm_eps = 1e-06


def destinations(expert_ids, copy_pick, slot_expert):
    slot_count = slot_expert.shape[0]
    slot_iota = jnp.arange(slot_count, dtype=jnp.int32)
    holders = expert_ids[:, :, None] == slot_expert[None, None, :]
    lower_slot = jnp.min(jnp.where(holders, slot_iota, slot_count), axis=2)
    upper_slot = jnp.max(jnp.where(holders, slot_iota, -1), axis=2)
    return jnp.where(copy_pick == 1, upper_slot, lower_slot)


def swap_tp(x):
    return lax.ppermute(x, "tp", perm=[(0, 1), (1, 0)])


def one_hot_rows(place, rows, tok_rows):
    top_count = place.shape[0] // tok_rows
    row_iota = jnp.arange(rows, dtype=jnp.int32)
    pick = place[:, None] == row_iota[None, :]
    return jnp.any(pick.reshape(top_count, tok_rows, rows), axis=0).astype(jnp.bfloat16)


def rows_split_experts(flat_target, flat_alive, position, normed_full, w_gate_up, w_down, capacity, tp_index):
    ep_count = lax.axis_size("ep")
    tok_rows, full_width = normed_full.shape
    half_width = full_width // 2
    share = -(-capacity // 2)
    rows = ep_count * share
    owner = position // share
    local = flat_target * share + position - owner * share
    mine = flat_alive & (owner == tp_index)
    spread = one_hot_rows(jnp.where(mine, local, -1), rows, tok_rows)
    filled = lax.dot_general(
        spread, normed_full, (((0,), (0,)), ((), ())), preferred_element_type=jnp.float32
    ).astype(jnp.bfloat16)
    arrived = lax.all_to_all(
        filled.reshape(ep_count, share, full_width // 128, 128),
        "ep",
        split_axis=0,
        concat_axis=0,
        tiled=True,
    ).reshape(rows, full_width)
    gate_up_other = swap_tp(w_gate_up[0])
    down_other = swap_tp(w_down[0])
    group_sums = []
    for gate_up, down in ((w_gate_up[0], w_down[0]), (gate_up_other, down_other)):
        pair = jnp.einsum("rd,gfd->rgf", arrived, gate_up, preferred_element_type=jnp.float32)
        hidden = (jax.nn.silu(pair[:, 0]) * pair[:, 1]).astype(jnp.bfloat16)
        group_sums.append(
            jnp.dot(hidden, down, preferred_element_type=jnp.float32).astype(jnp.bfloat16)
        )
    results = (group_sums[0].astype(jnp.float32) + group_sums[1].astype(jnp.float32)).astype(
        jnp.bfloat16
    )
    returned = lax.all_to_all(
        results.reshape(ep_count, share, full_width // 128, 128),
        "ep",
        split_axis=0,
        concat_axis=0,
        tiled=True,
    )
    tiles = half_width // 128
    own_half = lax.dynamic_slice_in_dim(returned, tp_index * tiles, tiles, 2)
    away_half = lax.dynamic_slice_in_dim(returned, (1 - tp_index) * tiles, tiles, 2)
    table = jnp.concatenate([own_half, swap_tp(away_half)], axis=0).reshape(2 * rows, tiles, 128)
    index = jnp.where(owner == tp_index, 0, rows) + local
    index = jnp.where(flat_alive, index, 0)
    return jnp.take(table, index, axis=0, mode="clip").astype(jnp.float32)


def units_split_experts(place, normed_part, w_gate_up, w_down, capacity, tp_index):
    ep_count = lax.axis_size("ep")
    tok_rows, slice_width = normed_part.shape
    slot_rows = ep_count * capacity
    spread = one_hot_rows(place, slot_rows, tok_rows)
    filled = lax.dot_general(
        spread, normed_part, (((0,), (0,)), ((), ())), preferred_element_type=jnp.float32
    ).astype(jnp.bfloat16)
    arrived = lax.all_to_all(
        filled.reshape(ep_count, capacity, slice_width // 128, 128),
        "ep",
        split_axis=0,
        concat_axis=0,
        tiled=True,
    )
    inputs = lax.all_gather(arrived.reshape(slot_rows, slice_width), "tp", axis=1, tiled=True)
    pair = jnp.einsum("rd,gfd->rgf", inputs, w_gate_up[0], preferred_element_type=jnp.float32)
    hidden = (jax.nn.silu(pair[:, 0]) * pair[:, 1]).astype(jnp.bfloat16)
    expert_terms = jnp.dot(hidden, w_down[0], preferred_element_type=jnp.float32).astype(
        jnp.bfloat16
    )
    results = lax.psum_scatter(expert_terms, "tp", scatter_dimension=1, tiled=True)
    returned = lax.all_to_all(
        results.reshape(ep_count, capacity, slice_width // 128, 128),
        "ep",
        split_axis=0,
        concat_axis=0,
        tiled=True,
    ).reshape(slot_rows, slice_width // 128, 128)
    return jnp.take(returned, jnp.maximum(place, 0), axis=0, mode="clip").astype(jnp.float32)


def body(
    attn_heads,
    w_out,
    resid_in,
    norm_gain,
    router_w,
    expert_ids,
    copy_pick,
    slot_expert,
    live_rows,
    w_gate_up,
    w_down,
):
    tp_count = lax.axis_size("tp")
    ep_count = lax.axis_size("ep")
    tp_index = lax.axis_index("tp")
    tok_rows, slice_width = resid_in.shape
    full_width = slice_width * tp_count
    top_count = expert_ids.shape[1]
    bound = max(2, 3 * tok_rows * top_count // (2 * (ep_count - ep_count // 16)))
    capacity = bound
    slot_rows = ep_count * capacity
    offset = tp_index * slice_width
    pair_tp = tp_count == 2

    proj = jnp.dot(attn_heads, w_out, preferred_element_type=jnp.float32)
    resid_full = lax.dynamic_update_slice_in_dim(
        jnp.zeros((tok_rows, full_width), jnp.float32), resid_in.astype(jnp.float32), offset, 1
    )
    terms = proj + resid_full
    if pair_tp:
        total = terms + swap_tp(terms)
    else:
        total = lax.psum(terms, "tp")
    stream_full = total.astype(jnp.bfloat16).astype(jnp.float32)
    mean_sq = jnp.mean(stream_full * stream_full, axis=1, keepdims=True)
    scale = lax.rsqrt(mean_sq + norm_eps)
    normed_full = (stream_full * scale * norm_gain.astype(jnp.float32)).astype(jnp.bfloat16)
    normed_part = lax.dynamic_slice_in_dim(normed_full, offset, slice_width, 1)
    stream_part = lax.dynamic_slice_in_dim(stream_full, offset, slice_width, 1)

    logits = jnp.dot(normed_full, router_w, preferred_element_type=jnp.float32)
    expert_iota = jnp.arange(router_w.shape[1], dtype=jnp.int32)
    chosen = jnp.sum(
        jnp.where(expert_ids[:, :, None] == expert_iota, logits[:, None, :], 0.0), axis=2
    )
    powers = jnp.exp(chosen)
    weights = powers / jnp.sum(powers, axis=1, keepdims=True)
    target = destinations(expert_ids, copy_pick, slot_expert)
    alive = jnp.arange(tok_rows, dtype=jnp.int32) < live_rows[0]

    target_kt = target.T
    alive_kt = jnp.broadcast_to(alive[None, :], target_kt.shape)
    flat_target = target_kt.reshape(-1)
    flat_alive = alive_kt.reshape(-1)
    slot_iota = jnp.arange(ep_count, dtype=jnp.int32)
    onehot = (flat_target[:, None] == slot_iota[None, :]) & flat_alive[:, None]
    ranks = jnp.cumsum(onehot.astype(jnp.int32), axis=0) - 1
    position = jnp.sum(jnp.where(onehot, ranks, 0), axis=1)

    if pair_tp:
        fetched = rows_split_experts(
            flat_target, flat_alive, position, normed_full, w_gate_up, w_down, capacity, tp_index
        )
    else:
        place = jnp.where(flat_alive, flat_target * capacity + position, -1)
        fetched = units_split_experts(
            place, normed_part, w_gate_up, w_down, capacity, tp_index
        )
    fetched = fetched.reshape(top_count, tok_rows, slice_width // 128, 128)
    scaled = (weights * alive[:, None].astype(jnp.float32)).T
    routed = jnp.sum(fetched * scaled[:, :, None, None], axis=0).reshape(tok_rows, slice_width)
    return (stream_part + routed).astype(jnp.bfloat16)


def solution(mesh):
    in_specs = (
        P("ep", "tp"),
        P("tp", None),
        P("ep", "tp"),
        P(),
        P(),
        P("ep", None),
        P("ep", None),
        P(),
        P("ep"),
        P("ep", None, "tp", None),
        P("ep", "tp", None),
    )
    out_specs = P("ep", "tp")
    return jax.shard_map(body, mesh=mesh, in_specs=in_specs, out_specs=out_specs, check_vma=False)
```

```python
import jax
import jax.numpy as jnp
from jax import lax
from jax.sharding import PartitionSpec as P

norm_eps = 1e-06


def destinations(expert_ids, copy_pick, slot_expert):
    slot_count = slot_expert.shape[0]
    slot_iota = jnp.arange(slot_count, dtype=jnp.int32)
    holders = expert_ids[:, :, None] == slot_expert[None, None, :]
    lower_slot = jnp.min(jnp.where(holders, slot_iota, slot_count), axis=2)
    upper_slot = jnp.max(jnp.where(holders, slot_iota, -1), axis=2)
    return jnp.where(copy_pick == 1, upper_slot, lower_slot)


def swap_tp(x):
    return lax.ppermute(x, "tp", perm=[(0, 1), (1, 0)])


def one_hot_rows(place, rows, tok_rows):
    top_count = place.shape[0] // tok_rows
    row_iota = jnp.arange(rows, dtype=jnp.int32)
    pick = place[:, None] == row_iota[None, :]
    return jnp.any(pick.reshape(top_count, tok_rows, rows), axis=0).astype(jnp.bfloat16)


def rows_split_experts(flat_target, flat_alive, position, normed_full, w_gate_up, w_down, capacity, tp_index):
    ep_count = lax.axis_size("ep")
    tok_rows, full_width = normed_full.shape
    half_width = full_width // 2
    share = -(-capacity // 2)
    owner = position // share
    mine = flat_alive & (owner == tp_index)
    gate_up_other = swap_tp(w_gate_up[0])
    down_other = swap_tp(w_down[0])
    tiles = half_width // 128
    within = position - owner * share
    first_size = -(-share // 2)
    chunks = [(0, first_size), (first_size, share - first_size)] if share > 1 else [(0, share)]
    own_parts = []
    away_parts = []
    index = jnp.zeros_like(position)
    base = 0
    for first, size in chunks:
        in_chunk = (within >= first) & (within < first + size)
        row = flat_target * size + within - first
        spread = one_hot_rows(jnp.where(mine & in_chunk, row, -1), ep_count * size, tok_rows)
        filled = lax.dot_general(
            spread, normed_full, (((0,), (0,)), ((), ())), preferred_element_type=jnp.float32
        ).astype(jnp.bfloat16)
        arrived = lax.all_to_all(
            filled.reshape(ep_count, size, full_width // 128, 128),
            "ep",
            split_axis=0,
            concat_axis=0,
            tiled=True,
        ).reshape(ep_count * size, full_width)
        group_sums = []
        for gate_up, down in ((w_gate_up[0], w_down[0]), (gate_up_other, down_other)):
            pair = jnp.einsum("rd,gfd->rgf", arrived, gate_up, preferred_element_type=jnp.float32)
            hidden = (jax.nn.silu(pair[:, 0]) * pair[:, 1]).astype(jnp.bfloat16)
            group_sums.append(
                jnp.dot(hidden, down, preferred_element_type=jnp.float32).astype(jnp.bfloat16)
            )
        results = (group_sums[0].astype(jnp.float32) + group_sums[1].astype(jnp.float32)).astype(
            jnp.bfloat16
        )
        returned = lax.all_to_all(
            results.reshape(ep_count, size, full_width // 128, 128),
            "ep",
            split_axis=0,
            concat_axis=0,
            tiled=True,
        )
        own_half = lax.dynamic_slice_in_dim(returned, tp_index * tiles, tiles, 2)
        away_half = lax.dynamic_slice_in_dim(returned, (1 - tp_index) * tiles, tiles, 2)
        own_parts.append(own_half.reshape(ep_count * size, tiles, 128))
        away_parts.append(swap_tp(away_half).reshape(ep_count * size, tiles, 128))
        index = jnp.where(in_chunk, base + row, index)
        base += ep_count * size
    table = jnp.concatenate(own_parts + away_parts, axis=0)
    index = jnp.where(owner == tp_index, 0, base) + index
    index = jnp.where(flat_alive, index, 0)
    return jnp.take(table, index, axis=0, mode="clip").astype(jnp.float32)


def units_split_experts(place, normed_part, w_gate_up, w_down, capacity, tp_index):
    ep_count = lax.axis_size("ep")
    tok_rows, slice_width = normed_part.shape
    slot_rows = ep_count * capacity
    spread = one_hot_rows(place, slot_rows, tok_rows)
    filled = lax.dot_general(
        spread, normed_part, (((0,), (0,)), ((), ())), preferred_element_type=jnp.float32
    ).astype(jnp.bfloat16)
    arrived = lax.all_to_all(
        filled.reshape(ep_count, capacity, slice_width // 128, 128),
        "ep",
        split_axis=0,
        concat_axis=0,
        tiled=True,
    )
    inputs = lax.all_gather(arrived.reshape(slot_rows, slice_width), "tp", axis=1, tiled=True)
    pair = jnp.einsum("rd,gfd->rgf", inputs, w_gate_up[0], preferred_element_type=jnp.float32)
    hidden = (jax.nn.silu(pair[:, 0]) * pair[:, 1]).astype(jnp.bfloat16)
    expert_terms = jnp.dot(hidden, w_down[0], preferred_element_type=jnp.float32).astype(
        jnp.bfloat16
    )
    results = lax.psum_scatter(expert_terms, "tp", scatter_dimension=1, tiled=True)
    returned = lax.all_to_all(
        results.reshape(ep_count, capacity, slice_width // 128, 128),
        "ep",
        split_axis=0,
        concat_axis=0,
        tiled=True,
    ).reshape(slot_rows, slice_width // 128, 128)
    return jnp.take(returned, jnp.maximum(place, 0), axis=0, mode="clip").astype(jnp.float32)


def body(
    attn_heads,
    w_out,
    resid_in,
    norm_gain,
    router_w,
    expert_ids,
    copy_pick,
    slot_expert,
    live_rows,
    w_gate_up,
    w_down,
):
    tp_count = lax.axis_size("tp")
    ep_count = lax.axis_size("ep")
    tp_index = lax.axis_index("tp")
    tok_rows, slice_width = resid_in.shape
    full_width = slice_width * tp_count
    top_count = expert_ids.shape[1]
    bound = max(2, 3 * tok_rows * top_count // (2 * (ep_count - ep_count // 16)))
    capacity = bound
    slot_rows = ep_count * capacity
    offset = tp_index * slice_width
    pair_tp = tp_count == 2

    proj = jnp.dot(attn_heads, w_out, preferred_element_type=jnp.float32)
    resid_full = lax.dynamic_update_slice_in_dim(
        jnp.zeros((tok_rows, full_width), jnp.float32), resid_in.astype(jnp.float32), offset, 1
    )
    terms = proj + resid_full
    if pair_tp:
        total = terms + swap_tp(terms)
    else:
        total = lax.psum(terms, "tp")
    stream_full = total.astype(jnp.bfloat16).astype(jnp.float32)
    mean_sq = jnp.mean(stream_full * stream_full, axis=1, keepdims=True)
    scale = lax.rsqrt(mean_sq + norm_eps)
    normed_full = (stream_full * scale * norm_gain.astype(jnp.float32)).astype(jnp.bfloat16)
    normed_part = lax.dynamic_slice_in_dim(normed_full, offset, slice_width, 1)
    stream_part = lax.dynamic_slice_in_dim(stream_full, offset, slice_width, 1)

    logits = jnp.dot(normed_full, router_w, preferred_element_type=jnp.float32)
    expert_iota = jnp.arange(router_w.shape[1], dtype=jnp.int32)
    chosen = jnp.sum(
        jnp.where(expert_ids[:, :, None] == expert_iota, logits[:, None, :], 0.0), axis=2
    )
    powers = jnp.exp(chosen)
    weights = powers / jnp.sum(powers, axis=1, keepdims=True)
    target = destinations(expert_ids, copy_pick, slot_expert)
    alive = jnp.arange(tok_rows, dtype=jnp.int32) < live_rows[0]

    target_kt = target.T
    alive_kt = jnp.broadcast_to(alive[None, :], target_kt.shape)
    flat_target = target_kt.reshape(-1)
    flat_alive = alive_kt.reshape(-1)
    slot_iota = jnp.arange(ep_count, dtype=jnp.int32)
    onehot = (flat_target[:, None] == slot_iota[None, :]) & flat_alive[:, None]
    ranks = jnp.cumsum(onehot.astype(jnp.int32), axis=0) - 1
    position = jnp.sum(jnp.where(onehot, ranks, 0), axis=1)

    if pair_tp:
        fetched = rows_split_experts(
            flat_target, flat_alive, position, normed_full, w_gate_up, w_down, capacity, tp_index
        )
    else:
        place = jnp.where(flat_alive, flat_target * capacity + position, -1)
        fetched = units_split_experts(
            place, normed_part, w_gate_up, w_down, capacity, tp_index
        )
    fetched = fetched.reshape(top_count, tok_rows, slice_width // 128, 128)
    scaled = (weights * alive[:, None].astype(jnp.float32)).T
    routed = jnp.sum(fetched * scaled[:, :, None, None], axis=0).reshape(tok_rows, slice_width)
    return (stream_part + routed).astype(jnp.bfloat16)


def solution(mesh):
    in_specs = (
        P("ep", "tp"),
        P("tp", None),
        P("ep", "tp"),
        P(),
        P(),
        P("ep", None),
        P("ep", None),
        P(),
        P("ep"),
        P("ep", None, "tp", None),
        P("ep", "tp", None),
    )
    out_specs = P("ep", "tp")
    return jax.shard_map(body, mesh=mesh, in_specs=in_specs, out_specs=out_specs, check_vma=False)
```

```python
import jax
import jax.numpy as jnp
from jax import lax
from jax.sharding import PartitionSpec as P

norm_eps = 1e-06


def destinations(expert_ids, copy_pick, slot_expert):
    slot_count = slot_expert.shape[0]
    slot_iota = jnp.arange(slot_count, dtype=jnp.int32)
    holders = expert_ids[:, :, None] == slot_expert[None, None, :]
    lower_slot = jnp.min(jnp.where(holders, slot_iota, slot_count), axis=2)
    upper_slot = jnp.max(jnp.where(holders, slot_iota, -1), axis=2)
    return jnp.where(copy_pick == 1, upper_slot, lower_slot)


def swap_tp(x):
    return lax.ppermute(x, "tp", perm=[(0, 1), (1, 0)])


def one_hot_rows(place, rows, tok_rows):
    top_count = place.shape[0] // tok_rows
    row_iota = jnp.arange(rows, dtype=jnp.int32)
    pick = place[:, None] == row_iota[None, :]
    return jnp.any(pick.reshape(top_count, tok_rows, rows), axis=0).astype(jnp.bfloat16)


def rows_split_experts(flat_target, flat_alive, position, normed_full, w_gate_up, w_down, capacity, tp_index):
    ep_count = lax.axis_size("ep")
    tok_rows, full_width = normed_full.shape
    half_width = full_width // 2
    share = -(-capacity // 2)
    rows = ep_count * share
    owner = position // share
    local = flat_target * share + position - owner * share
    mine = flat_alive & (owner == tp_index)
    spread = one_hot_rows(jnp.where(mine, local, -1), rows, tok_rows)
    filled = lax.dot_general(
        spread, normed_full, (((0,), (0,)), ((), ())), preferred_element_type=jnp.float32
    ).astype(jnp.bfloat16)
    arrived = lax.all_to_all(
        filled.reshape(ep_count, share, full_width // 128, 128),
        "ep",
        split_axis=0,
        concat_axis=0,
        tiled=True,
    ).reshape(rows, full_width)
    gate_up_other = swap_tp(w_gate_up[0])
    down_other = swap_tp(w_down[0])
    group_sums = []
    for gate_up, down in ((w_gate_up[0], w_down[0]), (gate_up_other, down_other)):
        pair = jnp.einsum("rd,gfd->rgf", arrived, gate_up, preferred_element_type=jnp.float32)
        hidden = (jax.nn.silu(pair[:, 0]) * pair[:, 1]).astype(jnp.bfloat16)
        group_sums.append(
            jnp.dot(hidden, down, preferred_element_type=jnp.float32).astype(jnp.bfloat16)
        )
    results = (group_sums[0].astype(jnp.float32) + group_sums[1].astype(jnp.float32)).astype(
        jnp.bfloat16
    )
    halves = results.reshape(ep_count, share, 2, half_width // 128, 128).transpose(0, 2, 1, 3, 4)
    returned = lax.all_to_all(
        halves.reshape(2 * ep_count, share, half_width // 128, 128),
        ("ep", "tp"),
        split_axis=0,
        concat_axis=0,
        tiled=True,
    ).reshape(2 * ep_count * share, half_width // 128, 128)
    index = (flat_target * 2 + owner) * share + position - owner * share
    index = jnp.where(flat_alive, index, 0)
    return jnp.take(returned, index, axis=0, mode="clip").astype(jnp.float32)


def units_split_experts(place, normed_part, w_gate_up, w_down, capacity, tp_index):
    ep_count = lax.axis_size("ep")
    tok_rows, slice_width = normed_part.shape
    slot_rows = ep_count * capacity
    spread = one_hot_rows(place, slot_rows, tok_rows)
    filled = lax.dot_general(
        spread, normed_part, (((0,), (0,)), ((), ())), preferred_element_type=jnp.float32
    ).astype(jnp.bfloat16)
    arrived = lax.all_to_all(
        filled.reshape(ep_count, capacity, slice_width // 128, 128),
        "ep",
        split_axis=0,
        concat_axis=0,
        tiled=True,
    )
    inputs = lax.all_gather(arrived.reshape(slot_rows, slice_width), "tp", axis=1, tiled=True)
    pair = jnp.einsum("rd,gfd->rgf", inputs, w_gate_up[0], preferred_element_type=jnp.float32)
    hidden = (jax.nn.silu(pair[:, 0]) * pair[:, 1]).astype(jnp.bfloat16)
    expert_terms = jnp.dot(hidden, w_down[0], preferred_element_type=jnp.float32).astype(
        jnp.bfloat16
    )
    results = lax.psum_scatter(expert_terms, "tp", scatter_dimension=1, tiled=True)
    returned = lax.all_to_all(
        results.reshape(ep_count, capacity, slice_width // 128, 128),
        "ep",
        split_axis=0,
        concat_axis=0,
        tiled=True,
    ).reshape(slot_rows, slice_width // 128, 128)
    return jnp.take(returned, jnp.maximum(place, 0), axis=0, mode="clip").astype(jnp.float32)


def body(
    attn_heads,
    w_out,
    resid_in,
    norm_gain,
    router_w,
    expert_ids,
    copy_pick,
    slot_expert,
    live_rows,
    w_gate_up,
    w_down,
):
    tp_count = lax.axis_size("tp")
    ep_count = lax.axis_size("ep")
    tp_index = lax.axis_index("tp")
    tok_rows, slice_width = resid_in.shape
    full_width = slice_width * tp_count
    top_count = expert_ids.shape[1]
    bound = max(2, 3 * tok_rows * top_count // (2 * (ep_count - ep_count // 16)))
    capacity = bound
    slot_rows = ep_count * capacity
    offset = tp_index * slice_width
    pair_tp = tp_count == 2

    proj = jnp.dot(attn_heads, w_out, preferred_element_type=jnp.float32)
    resid_full = lax.dynamic_update_slice_in_dim(
        jnp.zeros((tok_rows, full_width), jnp.float32), resid_in.astype(jnp.float32), offset, 1
    )
    terms = proj + resid_full
    if pair_tp:
        total = terms + swap_tp(terms)
    else:
        total = lax.psum(terms, "tp")
    stream_full = total.astype(jnp.bfloat16).astype(jnp.float32)
    mean_sq = jnp.mean(stream_full * stream_full, axis=1, keepdims=True)
    scale = lax.rsqrt(mean_sq + norm_eps)
    normed_full = (stream_full * scale * norm_gain.astype(jnp.float32)).astype(jnp.bfloat16)
    normed_part = lax.dynamic_slice_in_dim(normed_full, offset, slice_width, 1)
    stream_part = lax.dynamic_slice_in_dim(stream_full, offset, slice_width, 1)

    logits = jnp.dot(normed_full, router_w, preferred_element_type=jnp.float32)
    expert_iota = jnp.arange(router_w.shape[1], dtype=jnp.int32)
    chosen = jnp.sum(
        jnp.where(expert_ids[:, :, None] == expert_iota, logits[:, None, :], 0.0), axis=2
    )
    powers = jnp.exp(chosen)
    weights = powers / jnp.sum(powers, axis=1, keepdims=True)
    target = destinations(expert_ids, copy_pick, slot_expert)
    alive = jnp.arange(tok_rows, dtype=jnp.int32) < live_rows[0]

    target_kt = target.T
    alive_kt = jnp.broadcast_to(alive[None, :], target_kt.shape)
    flat_target = target_kt.reshape(-1)
    flat_alive = alive_kt.reshape(-1)
    slot_iota = jnp.arange(ep_count, dtype=jnp.int32)
    onehot = (flat_target[:, None] == slot_iota[None, :]) & flat_alive[:, None]
    ranks = jnp.cumsum(onehot.astype(jnp.int32), axis=0) - 1
    position = jnp.sum(jnp.where(onehot, ranks, 0), axis=1)

    if pair_tp:
        fetched = rows_split_experts(
            flat_target, flat_alive, position, normed_full, w_gate_up, w_down, capacity, tp_index
        )
    else:
        place = jnp.where(flat_alive, flat_target * capacity + position, -1)
        fetched = units_split_experts(
            place, normed_part, w_gate_up, w_down, capacity, tp_index
        )
    fetched = fetched.reshape(top_count, tok_rows, slice_width // 128, 128)
    scaled = (weights * alive[:, None].astype(jnp.float32)).T
    routed = jnp.sum(fetched * scaled[:, :, None, None], axis=0).reshape(tok_rows, slice_width)
    return (stream_part + routed).astype(jnp.bfloat16)


def solution(mesh):
    in_specs = (
        P("ep", "tp"),
        P("tp", None),
        P("ep", "tp"),
        P(),
        P(),
        P("ep", None),
        P("ep", None),
        P(),
        P("ep"),
        P("ep", None, "tp", None),
        P("ep", "tp", None),
    )
    out_specs = P("ep", "tp")
    return jax.shard_map(body, mesh=mesh, in_specs=in_specs, out_specs=out_specs, check_vma=False)
```

```python
import jax
import jax.numpy as jnp
from jax import lax
from jax.sharding import PartitionSpec as P

norm_eps = 1e-06


def destinations(expert_ids, copy_pick, slot_expert):
    slot_count = slot_expert.shape[0]
    slot_iota = jnp.arange(slot_count, dtype=jnp.int32)
    holders = expert_ids[:, :, None] == slot_expert[None, None, :]
    lower_slot = jnp.min(jnp.where(holders, slot_iota, slot_count), axis=2)
    upper_slot = jnp.max(jnp.where(holders, slot_iota, -1), axis=2)
    return jnp.where(copy_pick == 1, upper_slot, lower_slot)


def swap_tp(x):
    return lax.ppermute(x, "tp", perm=[(0, 1), (1, 0)])


def one_hot_rows(place, rows, tok_rows):
    top_count = place.shape[0] // tok_rows
    row_iota = jnp.arange(rows, dtype=jnp.int32)
    pick = place[:, None] == row_iota[None, :]
    return jnp.any(pick.reshape(top_count, tok_rows, rows), axis=0).astype(jnp.bfloat16)


def rows_split_experts(flat_target, flat_alive, position, normed_full, w_gate_up, w_down, capacity, tp_index):
    ep_count = lax.axis_size("ep")
    tok_rows, full_width = normed_full.shape
    half_width = full_width // 2
    share = -(-capacity // 2)
    rows = ep_count * share
    owner = position // share
    local = flat_target * share + position - owner * share
    mine = flat_alive & (owner == tp_index)
    spread = one_hot_rows(jnp.where(mine, local, -1), rows, tok_rows)
    filled = lax.dot_general(
        spread, normed_full, (((0,), (0,)), ((), ())), preferred_element_type=jnp.float32
    ).astype(jnp.bfloat16)
    arrived = lax.all_to_all(
        filled.reshape(ep_count, share, full_width // 128, 128),
        "ep",
        split_axis=0,
        concat_axis=0,
        tiled=True,
    ).reshape(rows, full_width)
    gate_up_other = swap_tp(w_gate_up[0])
    down_other = swap_tp(w_down[0])
    gate_up_all = jnp.concatenate([w_gate_up[0], gate_up_other], axis=1)
    down_all = jnp.concatenate([w_down[0], down_other], axis=0)
    pair = jnp.einsum("rd,gfd->rgf", arrived, gate_up_all, preferred_element_type=jnp.float32)
    hidden = (jax.nn.silu(pair[:, 0]) * pair[:, 1]).astype(jnp.bfloat16)
    results = jnp.dot(hidden, down_all, preferred_element_type=jnp.float32).astype(jnp.bfloat16)
    halves = results.reshape(ep_count, share, 2, half_width // 128, 128).transpose(0, 2, 1, 3, 4)
    returned = lax.all_to_all(
        halves.reshape(2 * ep_count, share, half_width // 128, 128),
        ("ep", "tp"),
        split_axis=0,
        concat_axis=0,
        tiled=True,
    ).reshape(2 * ep_count * share, half_width // 128, 128)
    index = (flat_target * 2 + owner) * share + position - owner * share
    index = jnp.where(flat_alive, index, 0)
    return jnp.take(returned, index, axis=0, mode="clip").astype(jnp.float32)


def units_split_experts(place, normed_part, w_gate_up, w_down, capacity, tp_index):
    ep_count = lax.axis_size("ep")
    tok_rows, slice_width = normed_part.shape
    slot_rows = ep_count * capacity
    spread = one_hot_rows(place, slot_rows, tok_rows)
    filled = lax.dot_general(
        spread, normed_part, (((0,), (0,)), ((), ())), preferred_element_type=jnp.float32
    ).astype(jnp.bfloat16)
    arrived = lax.all_to_all(
        filled.reshape(ep_count, capacity, slice_width // 128, 128),
        "ep",
        split_axis=0,
        concat_axis=0,
        tiled=True,
    )
    inputs = lax.all_gather(arrived.reshape(slot_rows, slice_width), "tp", axis=1, tiled=True)
    pair = jnp.einsum("rd,gfd->rgf", inputs, w_gate_up[0], preferred_element_type=jnp.float32)
    hidden = (jax.nn.silu(pair[:, 0]) * pair[:, 1]).astype(jnp.bfloat16)
    expert_terms = jnp.dot(hidden, w_down[0], preferred_element_type=jnp.float32).astype(
        jnp.bfloat16
    )
    results = lax.psum_scatter(expert_terms, "tp", scatter_dimension=1, tiled=True)
    returned = lax.all_to_all(
        results.reshape(ep_count, capacity, slice_width // 128, 128),
        "ep",
        split_axis=0,
        concat_axis=0,
        tiled=True,
    ).reshape(slot_rows, slice_width // 128, 128)
    return jnp.take(returned, jnp.maximum(place, 0), axis=0, mode="clip").astype(jnp.float32)


def body(
    attn_heads,
    w_out,
    resid_in,
    norm_gain,
    router_w,
    expert_ids,
    copy_pick,
    slot_expert,
    live_rows,
    w_gate_up,
    w_down,
):
    tp_count = lax.axis_size("tp")
    ep_count = lax.axis_size("ep")
    tp_index = lax.axis_index("tp")
    tok_rows, slice_width = resid_in.shape
    full_width = slice_width * tp_count
    top_count = expert_ids.shape[1]
    bound = max(2, 3 * tok_rows * top_count // (2 * (ep_count - ep_count // 16)))
    capacity = bound
    slot_rows = ep_count * capacity
    offset = tp_index * slice_width
    pair_tp = tp_count == 2

    proj = jnp.dot(attn_heads, w_out, preferred_element_type=jnp.float32)
    resid_full = lax.dynamic_update_slice_in_dim(
        jnp.zeros((tok_rows, full_width), jnp.float32), resid_in.astype(jnp.float32), offset, 1
    )
    terms = proj + resid_full
    if pair_tp:
        total = terms + swap_tp(terms)
    else:
        total = lax.psum(terms, "tp")
    stream_full = total.astype(jnp.bfloat16).astype(jnp.float32)
    mean_sq = jnp.mean(stream_full * stream_full, axis=1, keepdims=True)
    scale = lax.rsqrt(mean_sq + norm_eps)
    normed_full = (stream_full * scale * norm_gain.astype(jnp.float32)).astype(jnp.bfloat16)
    normed_part = lax.dynamic_slice_in_dim(normed_full, offset, slice_width, 1)
    stream_part = lax.dynamic_slice_in_dim(stream_full, offset, slice_width, 1)

    logits = jnp.dot(normed_full, router_w, preferred_element_type=jnp.float32)
    expert_iota = jnp.arange(router_w.shape[1], dtype=jnp.int32)
    chosen = jnp.sum(
        jnp.where(expert_ids[:, :, None] == expert_iota, logits[:, None, :], 0.0), axis=2
    )
    powers = jnp.exp(chosen)
    weights = powers / jnp.sum(powers, axis=1, keepdims=True)
    target = destinations(expert_ids, copy_pick, slot_expert)
    alive = jnp.arange(tok_rows, dtype=jnp.int32) < live_rows[0]

    target_kt = target.T
    alive_kt = jnp.broadcast_to(alive[None, :], target_kt.shape)
    flat_target = target_kt.reshape(-1)
    flat_alive = alive_kt.reshape(-1)
    slot_iota = jnp.arange(ep_count, dtype=jnp.int32)
    onehot = (flat_target[:, None] == slot_iota[None, :]) & flat_alive[:, None]
    ranks = jnp.cumsum(onehot.astype(jnp.int32), axis=0) - 1
    position = jnp.sum(jnp.where(onehot, ranks, 0), axis=1)

    if pair_tp:
        fetched = rows_split_experts(
            flat_target, flat_alive, position, normed_full, w_gate_up, w_down, capacity, tp_index
        )
    else:
        place = jnp.where(flat_alive, flat_target * capacity + position, -1)
        fetched = units_split_experts(
            place, normed_part, w_gate_up, w_down, capacity, tp_index
        )
    fetched = fetched.reshape(top_count, tok_rows, slice_width // 128, 128)
    scaled = (weights * alive[:, None].astype(jnp.float32)).T
    routed = jnp.sum(fetched * scaled[:, :, None, None], axis=0).reshape(tok_rows, slice_width)
    return (stream_part + routed).astype(jnp.bfloat16)


def solution(mesh):
    in_specs = (
        P("ep", "tp"),
        P("tp", None),
        P("ep", "tp"),
        P(),
        P(),
        P("ep", None),
        P("ep", None),
        P(),
        P("ep"),
        P("ep", None, "tp", None),
        P("ep", "tp", None),
    )
    out_specs = P("ep", "tp")
    return jax.shard_map(body, mesh=mesh, in_specs=in_specs, out_specs=out_specs, check_vma=False)
```

```python
import jax
import jax.numpy as jnp
from jax import lax
from jax.sharding import PartitionSpec as P

norm_eps = 1e-06


def destinations(expert_ids, copy_pick, slot_expert):
    slot_count = slot_expert.shape[0]
    slot_iota = jnp.arange(slot_count, dtype=jnp.int32)
    holders = expert_ids[:, :, None] == slot_expert[None, None, :]
    lower_slot = jnp.min(jnp.where(holders, slot_iota, slot_count), axis=2)
    upper_slot = jnp.max(jnp.where(holders, slot_iota, -1), axis=2)
    return jnp.where(copy_pick == 1, upper_slot, lower_slot)


def swap_tp(x):
    return lax.ppermute(x, "tp", perm=[(0, 1), (1, 0)])


def one_hot_rows(place, rows, tok_rows):
    top_count = place.shape[0] // tok_rows
    row_iota = jnp.arange(rows, dtype=jnp.int32)
    pick = place[:, None] == row_iota[None, :]
    return jnp.any(pick.reshape(top_count, tok_rows, rows), axis=0).astype(jnp.bfloat16)


def rows_split_experts(
    flat_target, flat_alive, position, normed_full, w_gate_up, w_down, capacity, tp_index, after
):
    ep_count = lax.axis_size("ep")
    tok_rows, full_width = normed_full.shape
    half_width = full_width // 2
    share = -(-capacity // 2)
    rows = ep_count * share
    owner = position // share
    local = flat_target * share + position - owner * share
    mine = flat_alive & (owner == tp_index)
    spread = one_hot_rows(jnp.where(mine, local, -1), rows, tok_rows)
    filled = lax.dot_general(
        spread, normed_full, (((0,), (0,)), ((), ())), preferred_element_type=jnp.float32
    ).astype(jnp.bfloat16)
    arrived = lax.all_to_all(
        filled.reshape(ep_count, share, full_width // 128, 128),
        "ep",
        split_axis=0,
        concat_axis=0,
        tiled=True,
    ).reshape(rows, full_width)
    gate_up_own, down_own, _ = lax.optimization_barrier((w_gate_up[0], w_down[0], after))
    gate_up_other = swap_tp(gate_up_own)
    down_other = swap_tp(down_own)
    gate_up_all = jnp.concatenate([gate_up_own, gate_up_other], axis=1)
    down_all = jnp.concatenate([down_own, down_other], axis=0)
    pair = jnp.einsum("rd,gfd->rgf", arrived, gate_up_all, preferred_element_type=jnp.float32)
    hidden = (jax.nn.silu(pair[:, 0]) * pair[:, 1]).astype(jnp.bfloat16)
    results = jnp.dot(hidden, down_all, preferred_element_type=jnp.float32).astype(jnp.bfloat16)
    halves = results.reshape(ep_count, share, 2, half_width // 128, 128).transpose(0, 2, 1, 3, 4)
    returned = lax.all_to_all(
        halves.reshape(2 * ep_count, share, half_width // 128, 128),
        ("ep", "tp"),
        split_axis=0,
        concat_axis=0,
        tiled=True,
    ).reshape(2 * ep_count * share, half_width // 128, 128)
    index = (flat_target * 2 + owner) * share + position - owner * share
    index = jnp.where(flat_alive, index, 0)
    return jnp.take(returned, index, axis=0, mode="clip").astype(jnp.float32)


def units_split_experts(place, normed_part, w_gate_up, w_down, capacity, tp_index):
    ep_count = lax.axis_size("ep")
    tok_rows, slice_width = normed_part.shape
    slot_rows = ep_count * capacity
    spread = one_hot_rows(place, slot_rows, tok_rows)
    filled = lax.dot_general(
        spread, normed_part, (((0,), (0,)), ((), ())), preferred_element_type=jnp.float32
    ).astype(jnp.bfloat16)
    arrived = lax.all_to_all(
        filled.reshape(ep_count, capacity, slice_width // 128, 128),
        "ep",
        split_axis=0,
        concat_axis=0,
        tiled=True,
    )
    inputs = lax.all_gather(arrived.reshape(slot_rows, slice_width), "tp", axis=1, tiled=True)
    pair = jnp.einsum("rd,gfd->rgf", inputs, w_gate_up[0], preferred_element_type=jnp.float32)
    hidden = (jax.nn.silu(pair[:, 0]) * pair[:, 1]).astype(jnp.bfloat16)
    expert_terms = jnp.dot(hidden, w_down[0], preferred_element_type=jnp.float32).astype(
        jnp.bfloat16
    )
    results = lax.psum_scatter(expert_terms, "tp", scatter_dimension=1, tiled=True)
    returned = lax.all_to_all(
        results.reshape(ep_count, capacity, slice_width // 128, 128),
        "ep",
        split_axis=0,
        concat_axis=0,
        tiled=True,
    ).reshape(slot_rows, slice_width // 128, 128)
    return jnp.take(returned, jnp.maximum(place, 0), axis=0, mode="clip").astype(jnp.float32)


def body(
    attn_heads,
    w_out,
    resid_in,
    norm_gain,
    router_w,
    expert_ids,
    copy_pick,
    slot_expert,
    live_rows,
    w_gate_up,
    w_down,
):
    tp_count = lax.axis_size("tp")
    ep_count = lax.axis_size("ep")
    tp_index = lax.axis_index("tp")
    tok_rows, slice_width = resid_in.shape
    full_width = slice_width * tp_count
    top_count = expert_ids.shape[1]
    bound = max(2, 3 * tok_rows * top_count // (2 * (ep_count - ep_count // 16)))
    capacity = bound
    slot_rows = ep_count * capacity
    offset = tp_index * slice_width
    pair_tp = tp_count == 2

    proj = jnp.dot(attn_heads, w_out, preferred_element_type=jnp.float32)
    resid_full = lax.dynamic_update_slice_in_dim(
        jnp.zeros((tok_rows, full_width), jnp.float32), resid_in.astype(jnp.float32), offset, 1
    )
    terms = proj + resid_full
    if pair_tp:
        total = terms + swap_tp(terms)
    else:
        total = lax.psum(terms, "tp")
    stream_full = total.astype(jnp.bfloat16).astype(jnp.float32)
    mean_sq = jnp.mean(stream_full * stream_full, axis=1, keepdims=True)
    scale = lax.rsqrt(mean_sq + norm_eps)
    normed_full = (stream_full * scale * norm_gain.astype(jnp.float32)).astype(jnp.bfloat16)
    normed_part = lax.dynamic_slice_in_dim(normed_full, offset, slice_width, 1)
    stream_part = lax.dynamic_slice_in_dim(stream_full, offset, slice_width, 1)

    logits = jnp.dot(normed_full, router_w, preferred_element_type=jnp.float32)
    expert_iota = jnp.arange(router_w.shape[1], dtype=jnp.int32)
    chosen = jnp.sum(
        jnp.where(expert_ids[:, :, None] == expert_iota, logits[:, None, :], 0.0), axis=2
    )
    powers = jnp.exp(chosen)
    weights = powers / jnp.sum(powers, axis=1, keepdims=True)
    target = destinations(expert_ids, copy_pick, slot_expert)
    alive = jnp.arange(tok_rows, dtype=jnp.int32) < live_rows[0]

    target_kt = target.T
    alive_kt = jnp.broadcast_to(alive[None, :], target_kt.shape)
    flat_target = target_kt.reshape(-1)
    flat_alive = alive_kt.reshape(-1)
    slot_iota = jnp.arange(ep_count, dtype=jnp.int32)
    onehot = (flat_target[:, None] == slot_iota[None, :]) & flat_alive[:, None]
    ranks = jnp.cumsum(onehot.astype(jnp.int32), axis=0) - 1
    position = jnp.sum(jnp.where(onehot, ranks, 0), axis=1)

    if pair_tp:
        fetched = rows_split_experts(
            flat_target, flat_alive, position, normed_full, w_gate_up, w_down, capacity, tp_index,
            total,
        )
    else:
        place = jnp.where(flat_alive, flat_target * capacity + position, -1)
        fetched = units_split_experts(
            place, normed_part, w_gate_up, w_down, capacity, tp_index
        )
    fetched = fetched.reshape(top_count, tok_rows, slice_width // 128, 128)
    scaled = (weights * alive[:, None].astype(jnp.float32)).T
    routed = jnp.sum(fetched * scaled[:, :, None, None], axis=0).reshape(tok_rows, slice_width)
    return (stream_part + routed).astype(jnp.bfloat16)


def solution(mesh):
    in_specs = (
        P("ep", "tp"),
        P("tp", None),
        P("ep", "tp"),
        P(),
        P(),
        P("ep", None),
        P("ep", None),
        P(),
        P("ep"),
        P("ep", None, "tp", None),
        P("ep", "tp", None),
    )
    out_specs = P("ep", "tp")
    return jax.shard_map(body, mesh=mesh, in_specs=in_specs, out_specs=out_specs, check_vma=False)
```

```python
import jax
import jax.numpy as jnp
from jax import lax
from jax.sharding import PartitionSpec as P

norm_eps = 1e-06


def destinations(expert_ids, copy_pick, slot_expert):
    slot_count = slot_expert.shape[0]
    slot_iota = jnp.arange(slot_count, dtype=jnp.int32)
    holders = expert_ids[:, :, None] == slot_expert[None, None, :]
    lower_slot = jnp.min(jnp.where(holders, slot_iota, slot_count), axis=2)
    upper_slot = jnp.max(jnp.where(holders, slot_iota, -1), axis=2)
    return jnp.where(copy_pick == 1, upper_slot, lower_slot)


def swap_tp(x):
    return lax.ppermute(x, "tp", perm=[(0, 1), (1, 0)])


def one_hot_rows(place, rows, tok_rows):
    top_count = place.shape[0] // tok_rows
    row_iota = jnp.arange(rows, dtype=jnp.int32)
    pick = place[:, None] == row_iota[None, :]
    return jnp.any(pick.reshape(top_count, tok_rows, rows), axis=0).astype(jnp.bfloat16)


def rows_split_experts(
    flat_target, flat_alive, position, normed_full, w_gate_up, w_down, capacity, tp_index, after
):
    ep_count = lax.axis_size("ep")
    tok_rows, full_width = normed_full.shape
    half_width = full_width // 2
    share = -(-capacity // 2)
    rows = ep_count * share
    owner = position // share
    local = flat_target * share + position - owner * share
    mine = flat_alive & (owner == tp_index)
    spread = one_hot_rows(jnp.where(mine, local, -1), rows, tok_rows)
    filled = lax.dot_general(
        spread, normed_full, (((0,), (0,)), ((), ())), preferred_element_type=jnp.float32
    ).astype(jnp.bfloat16)
    arrived = lax.all_to_all(
        filled.reshape(ep_count, share, full_width // 128, 128),
        "ep",
        split_axis=0,
        concat_axis=0,
        tiled=True,
    ).reshape(rows, full_width)
    gate_up_own, down_own, _ = lax.optimization_barrier((w_gate_up[0], w_down[0], after))
    gate_up_other = swap_tp(gate_up_own)
    down_other = swap_tp(down_own)
    gate_up_all = jnp.concatenate([gate_up_own, gate_up_other], axis=1)
    down_all = jnp.concatenate([down_own, down_other], axis=0)
    pair = jnp.einsum("rd,gfd->rgf", arrived, gate_up_all, preferred_element_type=jnp.float32)
    hidden = (jax.nn.silu(pair[:, 0]) * pair[:, 1]).astype(jnp.bfloat16)
    results = jnp.dot(hidden, down_all, preferred_element_type=jnp.float32).astype(jnp.bfloat16)
    halves = results.reshape(ep_count, share, 2, half_width // 128, 128).transpose(0, 2, 1, 3, 4)
    returned = lax.all_to_all(
        halves.reshape(2 * ep_count, share, half_width // 128, 128),
        ("ep", "tp"),
        split_axis=0,
        concat_axis=0,
        tiled=True,
    ).reshape(2 * ep_count * share, half_width // 128, 128)
    index = (flat_target * 2 + owner) * share + position - owner * share
    index = jnp.where(flat_alive, index, 0)
    return jnp.take(returned, index, axis=0, mode="clip").astype(jnp.float32)


def units_split_experts(place, normed_part, w_gate_up, w_down, capacity, tp_index):
    ep_count = lax.axis_size("ep")
    tok_rows, slice_width = normed_part.shape
    slot_rows = ep_count * capacity
    spread = one_hot_rows(place, slot_rows, tok_rows)
    filled = lax.dot_general(
        spread, normed_part, (((0,), (0,)), ((), ())), preferred_element_type=jnp.float32
    ).astype(jnp.bfloat16)
    arrived = lax.all_to_all(
        filled.reshape(ep_count, capacity, slice_width // 128, 128),
        "ep",
        split_axis=0,
        concat_axis=0,
        tiled=True,
    )
    inputs = lax.all_gather(arrived.reshape(slot_rows, slice_width), "tp", axis=1, tiled=True)
    pair = jnp.einsum("rd,gfd->rgf", inputs, w_gate_up[0], preferred_element_type=jnp.float32)
    hidden = (jax.nn.silu(pair[:, 0]) * pair[:, 1]).astype(jnp.bfloat16)
    expert_terms = jnp.dot(hidden, w_down[0], preferred_element_type=jnp.float32).astype(
        jnp.bfloat16
    )
    results = lax.psum_scatter(expert_terms, "tp", scatter_dimension=1, tiled=True)
    returned = lax.all_to_all(
        results.reshape(ep_count, capacity, slice_width // 128, 128),
        "ep",
        split_axis=0,
        concat_axis=0,
        tiled=True,
    ).reshape(slot_rows, slice_width // 128, 128)
    return jnp.take(returned, jnp.maximum(place, 0), axis=0, mode="clip").astype(jnp.float32)


def body(
    attn_heads,
    w_out,
    resid_in,
    norm_gain,
    router_w,
    expert_ids,
    copy_pick,
    slot_expert,
    live_rows,
    w_gate_up,
    w_down,
):
    tp_count = lax.axis_size("tp")
    ep_count = lax.axis_size("ep")
    tp_index = lax.axis_index("tp")
    tok_rows, slice_width = resid_in.shape
    full_width = slice_width * tp_count
    top_count = expert_ids.shape[1]
    bound = max(2, 3 * tok_rows * top_count // (2 * (ep_count - ep_count // 16)))
    capacity = bound
    slot_rows = ep_count * capacity
    offset = tp_index * slice_width
    pair_tp = tp_count == 2

    proj = jnp.dot(attn_heads, w_out, preferred_element_type=jnp.float32)
    resid_full = lax.dynamic_update_slice_in_dim(
        jnp.zeros((tok_rows, full_width), jnp.float32), resid_in.astype(jnp.float32), offset, 1
    )
    terms = proj + resid_full
    if pair_tp:
        total = terms + swap_tp(terms)
    else:
        total = lax.psum(terms, "tp")
    target = destinations(expert_ids, copy_pick, slot_expert)
    alive = jnp.arange(tok_rows, dtype=jnp.int32) < live_rows[0]

    target_kt = target.T
    alive_kt = jnp.broadcast_to(alive[None, :], target_kt.shape)
    flat_target = target_kt.reshape(-1)
    flat_alive = alive_kt.reshape(-1)
    slot_iota = jnp.arange(ep_count, dtype=jnp.int32)
    onehot = (flat_target[:, None] == slot_iota[None, :]) & flat_alive[:, None]
    ranks = jnp.cumsum(onehot.astype(jnp.int32), axis=0) - 1
    position = jnp.sum(jnp.where(onehot, ranks, 0), axis=1)

    total, position = lax.optimization_barrier((total, position))
    stream_full = total.astype(jnp.bfloat16).astype(jnp.float32)
    mean_sq = jnp.mean(stream_full * stream_full, axis=1, keepdims=True)
    scale = lax.rsqrt(mean_sq + norm_eps)
    normed_full = (stream_full * scale * norm_gain.astype(jnp.float32)).astype(jnp.bfloat16)
    normed_part = lax.dynamic_slice_in_dim(normed_full, offset, slice_width, 1)
    stream_part = lax.dynamic_slice_in_dim(stream_full, offset, slice_width, 1)

    logits = jnp.dot(normed_full, router_w, preferred_element_type=jnp.float32)
    expert_iota = jnp.arange(router_w.shape[1], dtype=jnp.int32)
    chosen = jnp.sum(
        jnp.where(expert_ids[:, :, None] == expert_iota, logits[:, None, :], 0.0), axis=2
    )
    powers = jnp.exp(chosen)
    weights = powers / jnp.sum(powers, axis=1, keepdims=True)
    if pair_tp:
        fetched = rows_split_experts(
            flat_target, flat_alive, position, normed_full, w_gate_up, w_down, capacity, tp_index,
            total,
        )
    else:
        place = jnp.where(flat_alive, flat_target * capacity + position, -1)
        fetched = units_split_experts(
            place, normed_part, w_gate_up, w_down, capacity, tp_index
        )
    fetched = fetched.reshape(top_count, tok_rows, slice_width // 128, 128)
    scaled = (weights * alive[:, None].astype(jnp.float32)).T
    routed = jnp.sum(fetched * scaled[:, :, None, None], axis=0).reshape(tok_rows, slice_width)
    return (stream_part + routed).astype(jnp.bfloat16)


def solution(mesh):
    in_specs = (
        P("ep", "tp"),
        P("tp", None),
        P("ep", "tp"),
        P(),
        P(),
        P("ep", None),
        P("ep", None),
        P(),
        P("ep"),
        P("ep", None, "tp", None),
        P("ep", "tp", None),
    )
    out_specs = P("ep", "tp")
    return jax.shard_map(body, mesh=mesh, in_specs=in_specs, out_specs=out_specs, check_vma=False)
```

```python
import jax
import jax.numpy as jnp
from jax import lax
from jax.sharding import PartitionSpec as P

norm_eps = 1e-06


def destinations(expert_ids, copy_pick, slot_expert):
    slot_count = slot_expert.shape[0]
    slot_iota = jnp.arange(slot_count, dtype=jnp.int32)
    holders = expert_ids[:, :, None] == slot_expert[None, None, :]
    lower_slot = jnp.min(jnp.where(holders, slot_iota, slot_count), axis=2)
    upper_slot = jnp.max(jnp.where(holders, slot_iota, -1), axis=2)
    return jnp.where(copy_pick == 1, upper_slot, lower_slot)


def swap_tp(x):
    return lax.ppermute(x, "tp", perm=[(0, 1), (1, 0)])


def one_hot_rows(place, rows, tok_rows):
    top_count = place.shape[0] // tok_rows
    row_iota = jnp.arange(rows, dtype=jnp.int32)
    pick = place[:, None] == row_iota[None, :]
    return jnp.any(pick.reshape(top_count, tok_rows, rows), axis=0).astype(jnp.bfloat16)


def rows_split_experts(
    flat_target, flat_alive, position, normed_full, w_gate_up, w_down, capacity, tp_index, after
):
    ep_count = lax.axis_size("ep")
    tok_rows, full_width = normed_full.shape
    half_width = full_width // 2
    share = -(-capacity // 2)
    rows = ep_count * share
    owner = position // share
    local = flat_target * share + position - owner * share
    mine = flat_alive & (owner == tp_index)
    spread = one_hot_rows(jnp.where(mine, local, -1), rows, tok_rows)
    filled = lax.dot_general(
        spread, normed_full, (((0,), (0,)), ((), ())), preferred_element_type=jnp.float32
    ).astype(jnp.bfloat16)
    arrived = lax.all_to_all(
        filled.reshape(ep_count, share, full_width // 128, 128),
        "ep",
        split_axis=0,
        concat_axis=0,
        tiled=True,
    ).reshape(rows, full_width)
    gate_up_own, down_own, _ = lax.optimization_barrier((w_gate_up[0], w_down[0], after))
    gate_up_other = swap_tp(gate_up_own)
    down_other = swap_tp(down_own)
    gate_up_all = jnp.concatenate([gate_up_own, gate_up_other], axis=1)
    down_all = jnp.concatenate([down_own, down_other], axis=0)
    pair = jnp.einsum("rd,gfd->rgf", arrived, gate_up_all, preferred_element_type=jnp.float32)
    hidden = (jax.nn.silu(pair[:, 0]) * pair[:, 1]).astype(jnp.bfloat16)
    results = jnp.dot(hidden, down_all, preferred_element_type=jnp.float32).astype(jnp.bfloat16)
    halves = results.reshape(ep_count, share, 2, half_width // 128, 128).transpose(0, 2, 1, 3, 4)
    returned = lax.all_to_all(
        halves.reshape(2 * ep_count, share, half_width // 128, 128),
        ("ep", "tp"),
        split_axis=0,
        concat_axis=0,
        tiled=True,
    ).reshape(2 * ep_count * share, half_width // 128, 128)
    index = (flat_target * 2 + owner) * share + position - owner * share
    index = jnp.where(flat_alive, index, 0)
    return jnp.take(returned, index, axis=0, mode="clip").astype(jnp.float32)


def units_split_experts(place, normed_part, w_gate_up, w_down, capacity, tp_index):
    ep_count = lax.axis_size("ep")
    tok_rows, slice_width = normed_part.shape
    slot_rows = ep_count * capacity
    spread = one_hot_rows(place, slot_rows, tok_rows)
    filled = lax.dot_general(
        spread, normed_part, (((0,), (0,)), ((), ())), preferred_element_type=jnp.float32
    ).astype(jnp.bfloat16)
    arrived = lax.all_to_all(
        filled.reshape(ep_count, capacity, slice_width // 128, 128),
        "ep",
        split_axis=0,
        concat_axis=0,
        tiled=True,
    )
    inputs = lax.all_gather(arrived.reshape(slot_rows, slice_width), "tp", axis=1, tiled=True)
    pair = jnp.einsum("rd,gfd->rgf", inputs, w_gate_up[0], preferred_element_type=jnp.float32)
    hidden = (jax.nn.silu(pair[:, 0]) * pair[:, 1]).astype(jnp.bfloat16)
    expert_terms = jnp.dot(hidden, w_down[0], preferred_element_type=jnp.float32).astype(
        jnp.bfloat16
    )
    results = lax.psum_scatter(expert_terms, "tp", scatter_dimension=1, tiled=True)
    returned = lax.all_to_all(
        results.reshape(ep_count, capacity, slice_width // 128, 128),
        "ep",
        split_axis=0,
        concat_axis=0,
        tiled=True,
    ).reshape(slot_rows, slice_width // 128, 128)
    return jnp.take(returned, jnp.maximum(place, 0), axis=0, mode="clip").astype(jnp.float32)


def body(
    attn_heads,
    w_out,
    resid_in,
    norm_gain,
    router_w,
    expert_ids,
    copy_pick,
    slot_expert,
    live_rows,
    w_gate_up,
    w_down,
):
    tp_count = lax.axis_size("tp")
    ep_count = lax.axis_size("ep")
    tp_index = lax.axis_index("tp")
    tok_rows, slice_width = resid_in.shape
    full_width = slice_width * tp_count
    top_count = expert_ids.shape[1]
    bound = max(2, 3 * tok_rows * top_count // (2 * (ep_count - ep_count // 16)))
    capacity = bound
    slot_rows = ep_count * capacity
    offset = tp_index * slice_width
    pair_tp = tp_count == 2

    proj = jnp.dot(attn_heads, w_out, preferred_element_type=jnp.float32)
    resid_full = lax.dynamic_update_slice_in_dim(
        jnp.zeros((tok_rows, full_width), jnp.float32), resid_in.astype(jnp.float32), offset, 1
    )
    terms = proj + resid_full
    if pair_tp:
        total = terms + swap_tp(terms.astype(jnp.bfloat16)).astype(jnp.float32)
    else:
        total = lax.psum(terms, "tp")
    target = destinations(expert_ids, copy_pick, slot_expert)
    alive = jnp.arange(tok_rows, dtype=jnp.int32) < live_rows[0]

    target_kt = target.T
    alive_kt = jnp.broadcast_to(alive[None, :], target_kt.shape)
    flat_target = target_kt.reshape(-1)
    flat_alive = alive_kt.reshape(-1)
    slot_iota = jnp.arange(ep_count, dtype=jnp.int32)
    onehot = (flat_target[:, None] == slot_iota[None, :]) & flat_alive[:, None]
    choice_iota = jnp.arange(flat_target.shape[0], dtype=jnp.int32)
    lower = (choice_iota[:, None] >= choice_iota[None, :]).astype(jnp.bfloat16)
    counts = jnp.dot(lower, onehot.astype(jnp.bfloat16), preferred_element_type=jnp.float32)
    ranks = counts.astype(jnp.int32) - 1
    position = jnp.sum(jnp.where(onehot, ranks, 0), axis=1)

    total, position = lax.optimization_barrier((total, position))
    stream_full = total.astype(jnp.bfloat16).astype(jnp.float32)
    mean_sq = jnp.mean(stream_full * stream_full, axis=1, keepdims=True)
    scale = lax.rsqrt(mean_sq + norm_eps)
    normed_full = (stream_full * scale * norm_gain.astype(jnp.float32)).astype(jnp.bfloat16)
    normed_part = lax.dynamic_slice_in_dim(normed_full, offset, slice_width, 1)
    stream_part = lax.dynamic_slice_in_dim(stream_full, offset, slice_width, 1)

    logits = jnp.dot(normed_full, router_w, preferred_element_type=jnp.float32)
    expert_iota = jnp.arange(router_w.shape[1], dtype=jnp.int32)
    chosen = jnp.sum(
        jnp.where(expert_ids[:, :, None] == expert_iota, logits[:, None, :], 0.0), axis=2
    )
    powers = jnp.exp(chosen)
    weights = powers / jnp.sum(powers, axis=1, keepdims=True)
    if pair_tp:
        fetched = rows_split_experts(
            flat_target, flat_alive, position, normed_full, w_gate_up, w_down, capacity, tp_index,
            total,
        )
    else:
        place = jnp.where(flat_alive, flat_target * capacity + position, -1)
        fetched = units_split_experts(
            place, normed_part, w_gate_up, w_down, capacity, tp_index
        )
    fetched = fetched.reshape(top_count, tok_rows, slice_width // 128, 128)
    scaled = (weights * alive[:, None].astype(jnp.float32)).T
    routed = jnp.sum(fetched * scaled[:, :, None, None], axis=0).reshape(tok_rows, slice_width)
    return (stream_part + routed).astype(jnp.bfloat16)


def solution(mesh):
    in_specs = (
        P("ep", "tp"),
        P("tp", None),
        P("ep", "tp"),
        P(),
        P(),
        P("ep", None),
        P("ep", None),
        P(),
        P("ep"),
        P("ep", None, "tp", None),
        P("ep", "tp", None),
    )
    out_specs = P("ep", "tp")
    return jax.shard_map(body, mesh=mesh, in_specs=in_specs, out_specs=out_specs, check_vma=False)
```

```python
import jax
import jax.numpy as jnp
from jax import lax
from jax.sharding import PartitionSpec as P

norm_eps = 1e-06


def destinations(expert_ids, copy_pick, slot_expert):
    slot_count = slot_expert.shape[0]
    slot_iota = jnp.arange(slot_count, dtype=jnp.int32)
    holders = expert_ids[:, :, None] == slot_expert[None, None, :]
    lower_slot = jnp.min(jnp.where(holders, slot_iota, slot_count), axis=2)
    upper_slot = jnp.max(jnp.where(holders, slot_iota, -1), axis=2)
    return jnp.where(copy_pick == 1, upper_slot, lower_slot)


def swap_tp(x):
    return lax.ppermute(x, "tp", perm=[(0, 1), (1, 0)])


def one_hot_rows(place, rows, tok_rows):
    top_count = place.shape[0] // tok_rows
    row_iota = jnp.arange(rows, dtype=jnp.int32)
    pick = place[:, None] == row_iota[None, :]
    return jnp.any(pick.reshape(top_count, tok_rows, rows), axis=0).astype(jnp.bfloat16)


def rows_split_experts(
    flat_target, flat_alive, position, normed_full, w_gate_up, w_down, capacity, tp_index, after
):
    ep_count = lax.axis_size("ep")
    tok_rows, full_width = normed_full.shape
    half_width = full_width // 2
    share = -(-capacity // 2)
    rows = ep_count * share
    owner = position // share
    local = flat_target * share + position - owner * share
    mine = flat_alive & (owner == tp_index)
    spread = one_hot_rows(jnp.where(mine, local, -1), rows, tok_rows)
    filled = lax.dot_general(
        spread, normed_full, (((0,), (0,)), ((), ())), preferred_element_type=jnp.float32
    ).astype(jnp.bfloat16)
    arrived = lax.all_to_all(
        filled.reshape(ep_count, share, full_width // 128, 128),
        "ep",
        split_axis=0,
        concat_axis=0,
        tiled=True,
    ).reshape(rows, full_width)
    gate_up_own, down_own, _ = lax.optimization_barrier((w_gate_up[0], w_down[0], after))
    gate_up_other = swap_tp(gate_up_own)
    down_other = swap_tp(down_own)
    gate_up_all = jnp.concatenate([gate_up_own, gate_up_other], axis=1)
    down_all = jnp.concatenate([down_own, down_other], axis=0)
    pair = jnp.einsum("rd,gfd->rgf", arrived, gate_up_all, preferred_element_type=jnp.float32)
    hidden = (jax.nn.silu(pair[:, 0]) * pair[:, 1]).astype(jnp.bfloat16)
    results = jnp.dot(hidden, down_all, preferred_element_type=jnp.float32).astype(jnp.bfloat16)
    halves = results.reshape(ep_count, share, 2, half_width // 128, 128).transpose(0, 2, 1, 3, 4)
    returned = lax.all_to_all(
        halves.reshape(2 * ep_count, share, half_width // 128, 128),
        ("ep", "tp"),
        split_axis=0,
        concat_axis=0,
        tiled=True,
    ).reshape(2 * ep_count * share, half_width // 128, 128)
    index = (flat_target * 2 + owner) * share + position - owner * share
    index = jnp.where(flat_alive, index, 0)
    return jnp.take(returned, index, axis=0, mode="clip").astype(jnp.float32)


def units_split_experts(place, normed_part, w_gate_up, w_down, capacity, tp_index):
    ep_count = lax.axis_size("ep")
    tok_rows, slice_width = normed_part.shape
    slot_rows = ep_count * capacity
    spread = one_hot_rows(place, slot_rows, tok_rows)
    filled = lax.dot_general(
        spread, normed_part, (((0,), (0,)), ((), ())), preferred_element_type=jnp.float32
    ).astype(jnp.bfloat16)
    arrived = lax.all_to_all(
        filled.reshape(ep_count, capacity, slice_width // 128, 128),
        "ep",
        split_axis=0,
        concat_axis=0,
        tiled=True,
    )
    inputs = lax.all_gather(arrived.reshape(slot_rows, slice_width), "tp", axis=1, tiled=True)
    pair = jnp.einsum("rd,gfd->rgf", inputs, w_gate_up[0], preferred_element_type=jnp.float32)
    hidden = (jax.nn.silu(pair[:, 0]) * pair[:, 1]).astype(jnp.bfloat16)
    expert_terms = jnp.dot(hidden, w_down[0], preferred_element_type=jnp.float32).astype(
        jnp.bfloat16
    )
    results = lax.psum_scatter(expert_terms, "tp", scatter_dimension=1, tiled=True)
    returned = lax.all_to_all(
        results.reshape(ep_count, capacity, slice_width // 128, 128),
        "ep",
        split_axis=0,
        concat_axis=0,
        tiled=True,
    ).reshape(slot_rows, slice_width // 128, 128)
    return jnp.take(returned, jnp.maximum(place, 0), axis=0, mode="clip").astype(jnp.float32)


def body(
    attn_heads,
    w_out,
    resid_in,
    norm_gain,
    router_w,
    expert_ids,
    copy_pick,
    slot_expert,
    live_rows,
    w_gate_up,
    w_down,
):
    tp_count = lax.axis_size("tp")
    ep_count = lax.axis_size("ep")
    tp_index = lax.axis_index("tp")
    tok_rows, slice_width = resid_in.shape
    full_width = slice_width * tp_count
    top_count = expert_ids.shape[1]
    bound = max(2, 3 * tok_rows * top_count // (2 * (ep_count - ep_count // 16)))
    capacity = bound
    slot_rows = ep_count * capacity
    offset = tp_index * slice_width
    pair_tp = tp_count == 2

    if pair_tp:
        resid_f = resid_in.astype(jnp.float32)
        sums = []
        for half in range(2):
            cols = w_out[:, half * slice_width : (half + 1) * slice_width]
            part = jnp.dot(attn_heads, cols, preferred_element_type=jnp.float32)
            part = part + jnp.where(tp_index == half, resid_f, 0.0)
            sums.append(part + swap_tp(part.astype(jnp.bfloat16)).astype(jnp.float32))
        total = jnp.concatenate(sums, axis=1)
    else:
        proj = jnp.dot(attn_heads, w_out, preferred_element_type=jnp.float32)
        resid_full = lax.dynamic_update_slice_in_dim(
            jnp.zeros((tok_rows, full_width), jnp.float32), resid_in.astype(jnp.float32), offset, 1
        )
        total = lax.psum(proj + resid_full, "tp")
    target = destinations(expert_ids, copy_pick, slot_expert)
    alive = jnp.arange(tok_rows, dtype=jnp.int32) < live_rows[0]

    target_kt = target.T
    alive_kt = jnp.broadcast_to(alive[None, :], target_kt.shape)
    flat_target = target_kt.reshape(-1)
    flat_alive = alive_kt.reshape(-1)
    slot_iota = jnp.arange(ep_count, dtype=jnp.int32)
    onehot = (flat_target[:, None] == slot_iota[None, :]) & flat_alive[:, None]
    choice_iota = jnp.arange(flat_target.shape[0], dtype=jnp.int32)
    lower = (choice_iota[:, None] >= choice_iota[None, :]).astype(jnp.bfloat16)
    counts = jnp.dot(lower, onehot.astype(jnp.bfloat16), preferred_element_type=jnp.float32)
    ranks = counts.astype(jnp.int32) - 1
    position = jnp.sum(jnp.where(onehot, ranks, 0), axis=1)

    total, position = lax.optimization_barrier((total, position))
    stream_full = total.astype(jnp.bfloat16).astype(jnp.float32)
    mean_sq = jnp.mean(stream_full * stream_full, axis=1, keepdims=True)
    scale = lax.rsqrt(mean_sq + norm_eps)
    normed_full = (stream_full * scale * norm_gain.astype(jnp.float32)).astype(jnp.bfloat16)
    normed_part = lax.dynamic_slice_in_dim(normed_full, offset, slice_width, 1)
    stream_part = lax.dynamic_slice_in_dim(stream_full, offset, slice_width, 1)

    logits = jnp.dot(normed_full, router_w, preferred_element_type=jnp.float32)
    expert_iota = jnp.arange(router_w.shape[1], dtype=jnp.int32)
    chosen = jnp.sum(
        jnp.where(expert_ids[:, :, None] == expert_iota, logits[:, None, :], 0.0), axis=2
    )
    powers = jnp.exp(chosen)
    weights = powers / jnp.sum(powers, axis=1, keepdims=True)
    if pair_tp:
        fetched = rows_split_experts(
            flat_target, flat_alive, position, normed_full, w_gate_up, w_down, capacity, tp_index,
            total,
        )
    else:
        place = jnp.where(flat_alive, flat_target * capacity + position, -1)
        fetched = units_split_experts(
            place, normed_part, w_gate_up, w_down, capacity, tp_index
        )
    fetched = fetched.reshape(top_count, tok_rows, slice_width // 128, 128)
    scaled = (weights * alive[:, None].astype(jnp.float32)).T
    routed = jnp.sum(fetched * scaled[:, :, None, None], axis=0).reshape(tok_rows, slice_width)
    return (stream_part + routed).astype(jnp.bfloat16)


def solution(mesh):
    in_specs = (
        P("ep", "tp"),
        P("tp", None),
        P("ep", "tp"),
        P(),
        P(),
        P("ep", None),
        P("ep", None),
        P(),
        P("ep"),
        P("ep", None, "tp", None),
        P("ep", "tp", None),
    )
    out_specs = P("ep", "tp")
    return jax.shard_map(body, mesh=mesh, in_specs=in_specs, out_specs=out_specs, check_vma=False)
```

```python
import jax
import jax.numpy as jnp
from jax import lax
from jax.sharding import PartitionSpec as P

norm_eps = 1e-06


def destinations(expert_ids, copy_pick, slot_expert):
    slot_count = slot_expert.shape[0]
    slot_iota = jnp.arange(slot_count, dtype=jnp.int32)
    holders = expert_ids[:, :, None] == slot_expert[None, None, :]
    lower_slot = jnp.min(jnp.where(holders, slot_iota, slot_count), axis=2)
    upper_slot = jnp.max(jnp.where(holders, slot_iota, -1), axis=2)
    return jnp.where(copy_pick == 1, upper_slot, lower_slot)


def swap_tp(x):
    return lax.ppermute(x, "tp", perm=[(0, 1), (1, 0)])


def one_hot_rows(place, rows, tok_rows):
    top_count = place.shape[0] // tok_rows
    row_iota = jnp.arange(rows, dtype=jnp.int32)
    pick = place[:, None] == row_iota[None, :]
    return jnp.any(pick.reshape(top_count, tok_rows, rows), axis=0).astype(jnp.bfloat16)


def rows_split_experts(
    flat_target, flat_alive, position, normed_full, w_gate_up, w_down, capacity, tp_index, after
):
    ep_count = lax.axis_size("ep")
    tok_rows, full_width = normed_full.shape
    half_width = full_width // 2
    share = -(-capacity // 2)
    rows = ep_count * share
    owner = position // share
    local = flat_target * share + position - owner * share
    mine = flat_alive & (owner == tp_index)
    spread = one_hot_rows(jnp.where(mine, local, -1), rows, tok_rows)
    filled = lax.dot_general(
        spread, normed_full, (((0,), (0,)), ((), ())), preferred_element_type=jnp.float32
    ).astype(jnp.bfloat16)
    arrived = lax.all_to_all(
        filled.reshape(ep_count, share, full_width // 128, 128),
        "ep",
        split_axis=0,
        concat_axis=0,
        tiled=True,
    ).reshape(rows, full_width // 128, 128)
    gate_up_own, down_own, _ = lax.optimization_barrier((w_gate_up[0], w_down[0], after))
    gate_up_other = swap_tp(gate_up_own)
    down_other = swap_tp(down_own)
    gate_up_all = jnp.concatenate([gate_up_own, gate_up_other], axis=1)
    down_all = jnp.concatenate([down_own, down_other], axis=0)
    gate_up_tiles = gate_up_all.reshape(2, -1, full_width // 128, 128)
    pair = jnp.einsum(
        "rjl,gfjl->rgf", arrived, gate_up_tiles, preferred_element_type=jnp.float32
    )
    hidden = (jax.nn.silu(pair[:, 0]) * pair[:, 1]).astype(jnp.bfloat16)
    results = jnp.dot(hidden, down_all, preferred_element_type=jnp.float32).astype(jnp.bfloat16)
    halves = results.reshape(ep_count, share, 2, half_width // 128, 128).transpose(0, 2, 1, 3, 4)
    returned = lax.all_to_all(
        halves.reshape(2 * ep_count, share, half_width // 128, 128),
        ("ep", "tp"),
        split_axis=0,
        concat_axis=0,
        tiled=True,
    ).reshape(2 * ep_count * share, half_width // 128, 128)
    index = (flat_target * 2 + owner) * share + position - owner * share
    index = jnp.where(flat_alive, index, 0)
    return jnp.take(returned, index, axis=0, mode="clip").astype(jnp.float32)


def units_split_experts(place, normed_part, w_gate_up, w_down, capacity, tp_index):
    ep_count = lax.axis_size("ep")
    tok_rows, slice_width = normed_part.shape
    slot_rows = ep_count * capacity
    spread = one_hot_rows(place, slot_rows, tok_rows)
    filled = lax.dot_general(
        spread, normed_part, (((0,), (0,)), ((), ())), preferred_element_type=jnp.float32
    ).astype(jnp.bfloat16)
    arrived = lax.all_to_all(
        filled.reshape(ep_count, capacity, slice_width // 128, 128),
        "ep",
        split_axis=0,
        concat_axis=0,
        tiled=True,
    )
    inputs = lax.all_gather(arrived.reshape(slot_rows, slice_width), "tp", axis=1, tiled=True)
    pair = jnp.einsum("rd,gfd->rgf", inputs, w_gate_up[0], preferred_element_type=jnp.float32)
    hidden = (jax.nn.silu(pair[:, 0]) * pair[:, 1]).astype(jnp.bfloat16)
    expert_terms = jnp.dot(hidden, w_down[0], preferred_element_type=jnp.float32).astype(
        jnp.bfloat16
    )
    results = lax.psum_scatter(expert_terms, "tp", scatter_dimension=1, tiled=True)
    returned = lax.all_to_all(
        results.reshape(ep_count, capacity, slice_width // 128, 128),
        "ep",
        split_axis=0,
        concat_axis=0,
        tiled=True,
    ).reshape(slot_rows, slice_width // 128, 128)
    return jnp.take(returned, jnp.maximum(place, 0), axis=0, mode="clip").astype(jnp.float32)


def body(
    attn_heads,
    w_out,
    resid_in,
    norm_gain,
    router_w,
    expert_ids,
    copy_pick,
    slot_expert,
    live_rows,
    w_gate_up,
    w_down,
):
    tp_count = lax.axis_size("tp")
    ep_count = lax.axis_size("ep")
    tp_index = lax.axis_index("tp")
    tok_rows, slice_width = resid_in.shape
    full_width = slice_width * tp_count
    top_count = expert_ids.shape[1]
    bound = max(2, 3 * tok_rows * top_count // (2 * (ep_count - ep_count // 16)))
    capacity = bound
    slot_rows = ep_count * capacity
    offset = tp_index * slice_width
    pair_tp = tp_count == 2

    proj = jnp.dot(attn_heads, w_out, preferred_element_type=jnp.float32)
    resid_full = lax.dynamic_update_slice_in_dim(
        jnp.zeros((tok_rows, full_width), jnp.float32), resid_in.astype(jnp.float32), offset, 1
    )
    terms = proj + resid_full
    if pair_tp:
        total = terms + swap_tp(terms.astype(jnp.bfloat16)).astype(jnp.float32)
    else:
        total = lax.psum(terms, "tp")
    target = destinations(expert_ids, copy_pick, slot_expert)
    alive = jnp.arange(tok_rows, dtype=jnp.int32) < live_rows[0]

    target_kt = target.T
    alive_kt = jnp.broadcast_to(alive[None, :], target_kt.shape)
    flat_target = target_kt.reshape(-1)
    flat_alive = alive_kt.reshape(-1)
    slot_iota = jnp.arange(ep_count, dtype=jnp.int32)
    onehot = (flat_target[:, None] == slot_iota[None, :]) & flat_alive[:, None]
    choice_iota = jnp.arange(flat_target.shape[0], dtype=jnp.int32)
    lower = (choice_iota[:, None] >= choice_iota[None, :]).astype(jnp.bfloat16)
    counts = jnp.dot(lower, onehot.astype(jnp.bfloat16), preferred_element_type=jnp.float32)
    ranks = counts.astype(jnp.int32) - 1
    position = jnp.sum(jnp.where(onehot, ranks, 0), axis=1)

    total, position = lax.optimization_barrier((total, position))
    stream_full = total.astype(jnp.bfloat16).astype(jnp.float32)
    mean_sq = jnp.mean(stream_full * stream_full, axis=1, keepdims=True)
    scale = lax.rsqrt(mean_sq + norm_eps)
    normed_full = (stream_full * scale * norm_gain.astype(jnp.float32)).astype(jnp.bfloat16)
    normed_part = lax.dynamic_slice_in_dim(normed_full, offset, slice_width, 1)
    stream_part = lax.dynamic_slice_in_dim(stream_full, offset, slice_width, 1)

    logits = jnp.dot(normed_full, router_w, preferred_element_type=jnp.float32)
    expert_iota = jnp.arange(router_w.shape[1], dtype=jnp.int32)
    chosen = jnp.sum(
        jnp.where(expert_ids[:, :, None] == expert_iota, logits[:, None, :], 0.0), axis=2
    )
    powers = jnp.exp(chosen)
    weights = powers / jnp.sum(powers, axis=1, keepdims=True)
    if pair_tp:
        fetched = rows_split_experts(
            flat_target, flat_alive, position, normed_full, w_gate_up, w_down, capacity, tp_index,
            total,
        )
    else:
        place = jnp.where(flat_alive, flat_target * capacity + position, -1)
        fetched = units_split_experts(
            place, normed_part, w_gate_up, w_down, capacity, tp_index
        )
    fetched = fetched.reshape(top_count, tok_rows, slice_width // 128, 128)
    scaled = (weights * alive[:, None].astype(jnp.float32)).T
    routed = jnp.sum(fetched * scaled[:, :, None, None], axis=0).reshape(tok_rows, slice_width)
    return (stream_part + routed).astype(jnp.bfloat16)


def solution(mesh):
    in_specs = (
        P("ep", "tp"),
        P("tp", None),
        P("ep", "tp"),
        P(),
        P(),
        P("ep", None),
        P("ep", None),
        P(),
        P("ep"),
        P("ep", None, "tp", None),
        P("ep", "tp", None),
    )
    out_specs = P("ep", "tp")
    return jax.shard_map(body, mesh=mesh, in_specs=in_specs, out_specs=out_specs, check_vma=False)
```

```python
import jax
import jax.numpy as jnp
from jax import lax
from jax.sharding import PartitionSpec as P

norm_eps = 1e-06


def destinations(expert_ids, copy_pick, slot_expert):
    slot_count = slot_expert.shape[0]
    slot_iota = jnp.arange(slot_count, dtype=jnp.int32)
    holders = expert_ids[:, :, None] == slot_expert[None, None, :]
    lower_slot = jnp.min(jnp.where(holders, slot_iota, slot_count), axis=2)
    upper_slot = jnp.max(jnp.where(holders, slot_iota, -1), axis=2)
    return jnp.where(copy_pick == 1, upper_slot, lower_slot)


def swap_tp(x):
    return lax.ppermute(x, "tp", perm=[(0, 1), (1, 0)])


def one_hot_rows(place, rows, tok_rows):
    top_count = place.shape[0] // tok_rows
    row_iota = jnp.arange(rows, dtype=jnp.int32)
    pick = place[:, None] == row_iota[None, :]
    return jnp.any(pick.reshape(top_count, tok_rows, rows), axis=0).astype(jnp.bfloat16)


def rows_split_experts(
    flat_target, flat_alive, position, normed_full, w_gate_up, w_down, capacity, tp_index, after
):
    ep_count = lax.axis_size("ep")
    tok_rows, full_width = normed_full.shape
    half_width = full_width // 2
    share = -(-capacity // 2)
    rows = ep_count * share
    owner = position // share
    local = flat_target * share + position - owner * share
    mine = flat_alive & (owner == tp_index)
    spread = one_hot_rows(jnp.where(mine, local, -1), rows, tok_rows)
    filled = lax.dot_general(
        spread, normed_full, (((0,), (0,)), ((), ())), preferred_element_type=jnp.float32
    ).astype(jnp.bfloat16)
    arrived = lax.all_to_all(
        filled.reshape(ep_count, share * full_width // 1024, 8, 128),
        "ep",
        split_axis=0,
        concat_axis=0,
        tiled=True,
    ).reshape(rows, full_width)
    gate_up_own, down_own, _ = lax.optimization_barrier((w_gate_up[0], w_down[0], after))
    gate_up_other = swap_tp(gate_up_own)
    down_other = swap_tp(down_own)
    gate_up_all = jnp.concatenate([gate_up_own, gate_up_other], axis=1)
    down_all = jnp.concatenate([down_own, down_other], axis=0)
    pair = jnp.einsum("rd,gfd->rgf", arrived, gate_up_all, preferred_element_type=jnp.float32)
    hidden = (jax.nn.silu(pair[:, 0]) * pair[:, 1]).astype(jnp.bfloat16)
    results = jnp.dot(hidden, down_all, preferred_element_type=jnp.float32).astype(jnp.bfloat16)
    halves = results.reshape(ep_count, share, 2, half_width // 128, 128).transpose(0, 2, 1, 3, 4)
    returned = lax.all_to_all(
        halves.reshape(2 * ep_count, share, half_width // 128, 128),
        ("ep", "tp"),
        split_axis=0,
        concat_axis=0,
        tiled=True,
    ).reshape(2 * ep_count * share, half_width // 128, 128)
    index = (flat_target * 2 + owner) * share + position - owner * share
    index = jnp.where(flat_alive, index, 0)
    return jnp.take(returned, index, axis=0, mode="clip").astype(jnp.float32)


def units_split_experts(place, normed_part, w_gate_up, w_down, capacity, tp_index):
    ep_count = lax.axis_size("ep")
    tok_rows, slice_width = normed_part.shape
    slot_rows = ep_count * capacity
    spread = one_hot_rows(place, slot_rows, tok_rows)
    filled = lax.dot_general(
        spread, normed_part, (((0,), (0,)), ((), ())), preferred_element_type=jnp.float32
    ).astype(jnp.bfloat16)
    arrived = lax.all_to_all(
        filled.reshape(ep_count, capacity, slice_width // 128, 128),
        "ep",
        split_axis=0,
        concat_axis=0,
        tiled=True,
    )
    inputs = lax.all_gather(arrived.reshape(slot_rows, slice_width), "tp", axis=1, tiled=True)
    pair = jnp.einsum("rd,gfd->rgf", inputs, w_gate_up[0], preferred_element_type=jnp.float32)
    hidden = (jax.nn.silu(pair[:, 0]) * pair[:, 1]).astype(jnp.bfloat16)
    expert_terms = jnp.dot(hidden, w_down[0], preferred_element_type=jnp.float32).astype(
        jnp.bfloat16
    )
    results = lax.psum_scatter(expert_terms, "tp", scatter_dimension=1, tiled=True)
    returned = lax.all_to_all(
        results.reshape(ep_count, capacity, slice_width // 128, 128),
        "ep",
        split_axis=0,
        concat_axis=0,
        tiled=True,
    ).reshape(slot_rows, slice_width // 128, 128)
    return jnp.take(returned, jnp.maximum(place, 0), axis=0, mode="clip").astype(jnp.float32)


def body(
    attn_heads,
    w_out,
    resid_in,
    norm_gain,
    router_w,
    expert_ids,
    copy_pick,
    slot_expert,
    live_rows,
    w_gate_up,
    w_down,
):
    tp_count = lax.axis_size("tp")
    ep_count = lax.axis_size("ep")
    tp_index = lax.axis_index("tp")
    tok_rows, slice_width = resid_in.shape
    full_width = slice_width * tp_count
    top_count = expert_ids.shape[1]
    bound = max(2, 3 * tok_rows * top_count // (2 * (ep_count - ep_count // 16)))
    capacity = bound
    slot_rows = ep_count * capacity
    offset = tp_index * slice_width
    pair_tp = tp_count == 2

    proj = jnp.dot(attn_heads, w_out, preferred_element_type=jnp.float32)
    resid_full = lax.dynamic_update_slice_in_dim(
        jnp.zeros((tok_rows, full_width), jnp.float32), resid_in.astype(jnp.float32), offset, 1
    )
    terms = proj + resid_full
    if pair_tp:
        total = terms + swap_tp(terms.astype(jnp.bfloat16)).astype(jnp.float32)
    else:
        total = lax.psum(terms, "tp")
    target = destinations(expert_ids, copy_pick, slot_expert)
    alive = jnp.arange(tok_rows, dtype=jnp.int32) < live_rows[0]

    target_kt = target.T
    alive_kt = jnp.broadcast_to(alive[None, :], target_kt.shape)
    flat_target = target_kt.reshape(-1)
    flat_alive = alive_kt.reshape(-1)
    slot_iota = jnp.arange(ep_count, dtype=jnp.int32)
    onehot = (flat_target[:, None] == slot_iota[None, :]) & flat_alive[:, None]
    choice_iota = jnp.arange(flat_target.shape[0], dtype=jnp.int32)
    lower = (choice_iota[:, None] >= choice_iota[None, :]).astype(jnp.bfloat16)
    counts = jnp.dot(lower, onehot.astype(jnp.bfloat16), preferred_element_type=jnp.float32)
    ranks = counts.astype(jnp.int32) - 1
    position = jnp.sum(jnp.where(onehot, ranks, 0), axis=1)

    total, position = lax.optimization_barrier((total, position))
    stream_full = total.astype(jnp.bfloat16).astype(jnp.float32)
    mean_sq = jnp.mean(stream_full * stream_full, axis=1, keepdims=True)
    scale = lax.rsqrt(mean_sq + norm_eps)
    normed_full = (stream_full * scale * norm_gain.astype(jnp.float32)).astype(jnp.bfloat16)
    normed_part = lax.dynamic_slice_in_dim(normed_full, offset, slice_width, 1)
    stream_part = lax.dynamic_slice_in_dim(stream_full, offset, slice_width, 1)

    logits = jnp.dot(normed_full, router_w, preferred_element_type=jnp.float32)
    expert_iota = jnp.arange(router_w.shape[1], dtype=jnp.int32)
    chosen = jnp.sum(
        jnp.where(expert_ids[:, :, None] == expert_iota, logits[:, None, :], 0.0), axis=2
    )
    powers = jnp.exp(chosen)
    weights = powers / jnp.sum(powers, axis=1, keepdims=True)
    if pair_tp:
        fetched = rows_split_experts(
            flat_target, flat_alive, position, normed_full, w_gate_up, w_down, capacity, tp_index,
            total,
        )
    else:
        place = jnp.where(flat_alive, flat_target * capacity + position, -1)
        fetched = units_split_experts(
            place, normed_part, w_gate_up, w_down, capacity, tp_index
        )
    fetched = fetched.reshape(top_count, tok_rows, slice_width // 128, 128)
    scaled = (weights * alive[:, None].astype(jnp.float32)).T
    routed = jnp.sum(fetched * scaled[:, :, None, None], axis=0).reshape(tok_rows, slice_width)
    return (stream_part + routed).astype(jnp.bfloat16)


def solution(mesh):
    in_specs = (
        P("ep", "tp"),
        P("tp", None),
        P("ep", "tp"),
        P(),
        P(),
        P("ep", None),
        P("ep", None),
        P(),
        P("ep"),
        P("ep", None, "tp", None),
        P("ep", "tp", None),
    )
    out_specs = P("ep", "tp")
    return jax.shard_map(body, mesh=mesh, in_specs=in_specs, out_specs=out_specs, check_vma=False)
```

```python
import jax
import jax.numpy as jnp
from jax import lax
from jax.sharding import PartitionSpec as P

norm_eps = 1e-06


def destinations(expert_ids, copy_pick, slot_expert):
    slot_count = slot_expert.shape[0]
    slot_iota = jnp.arange(slot_count, dtype=jnp.int32)
    holders = expert_ids[:, :, None] == slot_expert[None, None, :]
    lower_slot = jnp.min(jnp.where(holders, slot_iota, slot_count), axis=2)
    upper_slot = jnp.max(jnp.where(holders, slot_iota, -1), axis=2)
    return jnp.where(copy_pick == 1, upper_slot, lower_slot)


def swap_tp(x):
    return lax.ppermute(x, "tp", perm=[(0, 1), (1, 0)])


def one_hot_rows(place, rows, tok_rows):
    top_count = place.shape[0] // tok_rows
    row_iota = jnp.arange(rows, dtype=jnp.int32)
    pick = place[:, None] == row_iota[None, :]
    return jnp.any(pick.reshape(top_count, tok_rows, rows), axis=0).astype(jnp.bfloat16)


def rows_split_experts(
    flat_target, flat_alive, position, normed_full, w_gate_up, w_down, capacity, tp_index, after
):
    ep_count = lax.axis_size("ep")
    tok_rows, full_width = normed_full.shape
    half_width = full_width // 2
    share = -(-capacity // 2)
    rows = ep_count * share
    owner = position // share
    local = flat_target * share + position - owner * share
    mine = flat_alive & (owner == tp_index)
    spread = one_hot_rows(jnp.where(mine, local, -1), rows, tok_rows)
    filled = lax.dot_general(
        spread, normed_full, (((0,), (0,)), ((), ())), preferred_element_type=jnp.float32
    ).astype(jnp.bfloat16)
    arrived = lax.all_to_all(
        filled.reshape(ep_count, share, full_width // 128, 128),
        "ep",
        split_axis=0,
        concat_axis=0,
        tiled=True,
    ).reshape(rows, full_width)
    gate_up_own, down_own, _ = lax.optimization_barrier((w_gate_up[0], w_down[0], after))
    gate_up_other = swap_tp(gate_up_own)
    down_other = swap_tp(down_own)
    gate_up_all = jnp.concatenate([gate_up_own, gate_up_other], axis=1)
    down_all = jnp.concatenate([down_own, down_other], axis=0)
    pair = jnp.einsum("rd,gfd->rgf", arrived, gate_up_all, preferred_element_type=jnp.float32)
    hidden = (jax.nn.silu(pair[:, 0]) * pair[:, 1]).astype(jnp.bfloat16)
    results = jnp.dot(hidden, down_all, preferred_element_type=jnp.float32).astype(jnp.bfloat16)
    halves = results.reshape(ep_count, share, 2, half_width // 128, 128).transpose(0, 2, 1, 3, 4)
    returned = lax.all_to_all(
        halves.reshape(2 * ep_count, share, half_width // 128, 128),
        ("ep", "tp"),
        split_axis=0,
        concat_axis=0,
        tiled=True,
    ).reshape(2 * ep_count * share, half_width // 128, 128)
    index = (flat_target * 2 + owner) * share + position - owner * share
    index = jnp.where(flat_alive, index, 0)
    return jnp.take(returned, index, axis=0, mode="clip").astype(jnp.float32)


def units_split_experts(place, normed_part, w_gate_up, w_down, capacity, tp_index):
    ep_count = lax.axis_size("ep")
    tok_rows, slice_width = normed_part.shape
    slot_rows = ep_count * capacity
    spread = one_hot_rows(place, slot_rows, tok_rows)
    filled = lax.dot_general(
        spread, normed_part, (((0,), (0,)), ((), ())), preferred_element_type=jnp.float32
    ).astype(jnp.bfloat16)
    arrived = lax.all_to_all(
        filled.reshape(ep_count, capacity, slice_width // 128, 128),
        "ep",
        split_axis=0,
        concat_axis=0,
        tiled=True,
    )
    inputs = lax.all_gather(arrived.reshape(slot_rows, slice_width), "tp", axis=1, tiled=True)
    pair = jnp.einsum("rd,gfd->rgf", inputs, w_gate_up[0], preferred_element_type=jnp.float32)
    hidden = (jax.nn.silu(pair[:, 0]) * pair[:, 1]).astype(jnp.bfloat16)
    expert_terms = jnp.dot(hidden, w_down[0], preferred_element_type=jnp.float32).astype(
        jnp.bfloat16
    )
    results = lax.psum_scatter(expert_terms, "tp", scatter_dimension=1, tiled=True)
    returned = lax.all_to_all(
        results.reshape(ep_count, capacity, slice_width // 128, 128),
        "ep",
        split_axis=0,
        concat_axis=0,
        tiled=True,
    ).reshape(slot_rows, slice_width // 128, 128)
    return jnp.take(returned, jnp.maximum(place, 0), axis=0, mode="clip").astype(jnp.float32)


def body(
    attn_heads,
    w_out,
    resid_in,
    norm_gain,
    router_w,
    expert_ids,
    copy_pick,
    slot_expert,
    live_rows,
    w_gate_up,
    w_down,
):
    tp_count = lax.axis_size("tp")
    ep_count = lax.axis_size("ep")
    tp_index = lax.axis_index("tp")
    tok_rows, slice_width = resid_in.shape
    full_width = slice_width * tp_count
    top_count = expert_ids.shape[1]
    bound = max(2, 3 * tok_rows * top_count // (2 * (ep_count - ep_count // 16)))
    capacity = bound
    slot_rows = ep_count * capacity
    offset = tp_index * slice_width
    pair_tp = tp_count == 2

    heads = jnp.where(live_rows[0] > 0, attn_heads, jnp.zeros_like(attn_heads))
    proj = jnp.dot(heads, w_out, preferred_element_type=jnp.float32)
    resid_full = lax.dynamic_update_slice_in_dim(
        jnp.zeros((tok_rows, full_width), jnp.float32), resid_in.astype(jnp.float32), offset, 1
    )
    terms = proj + resid_full
    if pair_tp:
        total = terms + swap_tp(terms.astype(jnp.bfloat16)).astype(jnp.float32)
    else:
        total = lax.psum(terms, "tp")
    target = destinations(expert_ids, copy_pick, slot_expert)
    alive = jnp.arange(tok_rows, dtype=jnp.int32) < live_rows[0]

    target_kt = target.T
    alive_kt = jnp.broadcast_to(alive[None, :], target_kt.shape)
    flat_target = target_kt.reshape(-1)
    flat_alive = alive_kt.reshape(-1)
    slot_iota = jnp.arange(ep_count, dtype=jnp.int32)
    onehot = (flat_target[:, None] == slot_iota[None, :]) & flat_alive[:, None]
    choice_iota = jnp.arange(flat_target.shape[0], dtype=jnp.int32)
    lower = (choice_iota[:, None] >= choice_iota[None, :]).astype(jnp.bfloat16)
    counts = jnp.dot(lower, onehot.astype(jnp.bfloat16), preferred_element_type=jnp.float32)
    ranks = counts.astype(jnp.int32) - 1
    position = jnp.sum(jnp.where(onehot, ranks, 0), axis=1)

    total, position = lax.optimization_barrier((total, position))
    stream_full = total.astype(jnp.bfloat16).astype(jnp.float32)
    mean_sq = jnp.mean(stream_full * stream_full, axis=1, keepdims=True)
    scale = lax.rsqrt(mean_sq + norm_eps)
    normed_full = (stream_full * scale * norm_gain.astype(jnp.float32)).astype(jnp.bfloat16)
    normed_part = lax.dynamic_slice_in_dim(normed_full, offset, slice_width, 1)
    stream_part = lax.dynamic_slice_in_dim(stream_full, offset, slice_width, 1)

    logits = jnp.dot(normed_full, router_w, preferred_element_type=jnp.float32)
    expert_iota = jnp.arange(router_w.shape[1], dtype=jnp.int32)
    chosen = jnp.sum(
        jnp.where(expert_ids[:, :, None] == expert_iota, logits[:, None, :], 0.0), axis=2
    )
    powers = jnp.exp(chosen)
    weights = powers / jnp.sum(powers, axis=1, keepdims=True)
    if pair_tp:
        fetched = rows_split_experts(
            flat_target, flat_alive, position, normed_full, w_gate_up, w_down, capacity, tp_index,
            total,
        )
    else:
        place = jnp.where(flat_alive, flat_target * capacity + position, -1)
        fetched = units_split_experts(
            place, normed_part, w_gate_up, w_down, capacity, tp_index
        )
    fetched = fetched.reshape(top_count, tok_rows, slice_width // 128, 128)
    scaled = (weights * alive[:, None].astype(jnp.float32)).T
    routed = jnp.sum(fetched * scaled[:, :, None, None], axis=0).reshape(tok_rows, slice_width)
    return (stream_part + routed).astype(jnp.bfloat16)


def solution(mesh):
    in_specs = (
        P("ep", "tp"),
        P("tp", None),
        P("ep", "tp"),
        P(),
        P(),
        P("ep", None),
        P("ep", None),
        P(),
        P("ep"),
        P("ep", None, "tp", None),
        P("ep", "tp", None),
    )
    out_specs = P("ep", "tp")
    return jax.shard_map(body, mesh=mesh, in_specs=in_specs, out_specs=out_specs, check_vma=False)
```

```python
import jax
import jax.numpy as jnp
from jax import lax
from jax.sharding import PartitionSpec as P

norm_eps = 1e-06


def destinations(expert_ids, copy_pick, slot_expert):
    slot_count = slot_expert.shape[0]
    slot_iota = jnp.arange(slot_count, dtype=jnp.int32)
    holders = expert_ids[:, :, None] == slot_expert[None, None, :]
    lower_slot = jnp.min(jnp.where(holders, slot_iota, slot_count), axis=2)
    upper_slot = jnp.max(jnp.where(holders, slot_iota, -1), axis=2)
    return jnp.where(copy_pick == 1, upper_slot, lower_slot)


def swap_tp(x):
    return lax.ppermute(x, "tp", perm=[(0, 1), (1, 0)])


def one_hot_rows(place, rows, tok_rows):
    top_count = place.shape[0] // tok_rows
    row_iota = jnp.arange(rows, dtype=jnp.int32)
    pick = place[:, None] == row_iota[None, :]
    return jnp.any(pick.reshape(top_count, tok_rows, rows), axis=0).astype(jnp.bfloat16)


def rows_split_experts(
    flat_target, flat_alive, position, normed_full, w_gate_up, w_down, capacity, tp_index, after
):
    ep_count = lax.axis_size("ep")
    tok_rows, full_width = normed_full.shape
    half_width = full_width // 2
    share = -(-capacity // 2)
    rows = ep_count * share
    owner = position // share
    local = flat_target * share + position - owner * share
    mine = flat_alive & (owner == tp_index)
    spread = one_hot_rows(jnp.where(mine, local, -1), rows, tok_rows)
    filled = lax.dot_general(
        spread, normed_full, (((0,), (0,)), ((), ())), preferred_element_type=jnp.float32
    ).astype(jnp.bfloat16)
    arrived = lax.all_to_all(
        filled.reshape(ep_count, share, full_width // 128, 128),
        "ep",
        split_axis=0,
        concat_axis=0,
        tiled=True,
    ).reshape(rows, full_width)
    gate_up_own, down_own, _ = lax.optimization_barrier((w_gate_up[0], w_down[0], after))
    gate_up_other = swap_tp(gate_up_own)
    down_other = swap_tp(down_own)
    gate_up_all = jnp.concatenate([gate_up_own, gate_up_other], axis=1)
    down_all = jnp.concatenate([down_own, down_other], axis=0)
    pair = jnp.einsum("rd,gfd->rgf", arrived, gate_up_all, preferred_element_type=jnp.float32)
    hidden = (jax.nn.silu(pair[:, 0]) * pair[:, 1]).astype(jnp.bfloat16)
    results = jnp.dot(hidden, down_all, preferred_element_type=jnp.float32).astype(jnp.bfloat16)
    halves = results.reshape(ep_count, share, 2, half_width // 128, 128).transpose(0, 2, 1, 3, 4)
    returned = lax.all_to_all(
        halves.reshape(2 * ep_count, share, half_width // 128, 128),
        ("ep", "tp"),
        split_axis=0,
        concat_axis=0,
        tiled=True,
    ).reshape(2 * ep_count * share, half_width // 128, 128)
    index = (flat_target * 2 + owner) * share + position - owner * share
    index = jnp.where(flat_alive, index, 0)
    return jnp.take(returned, index, axis=0, mode="clip").astype(jnp.float32)


def units_split_experts(place, normed_part, w_gate_up, w_down, capacity, tp_index):
    ep_count = lax.axis_size("ep")
    tok_rows, slice_width = normed_part.shape
    slot_rows = ep_count * capacity
    spread = one_hot_rows(place, slot_rows, tok_rows)
    filled = lax.dot_general(
        spread, normed_part, (((0,), (0,)), ((), ())), preferred_element_type=jnp.float32
    ).astype(jnp.bfloat16)
    arrived = lax.all_to_all(
        filled.reshape(ep_count, capacity, slice_width // 128, 128),
        "ep",
        split_axis=0,
        concat_axis=0,
        tiled=True,
    )
    inputs = lax.all_gather(arrived.reshape(slot_rows, slice_width), "tp", axis=1, tiled=True)
    pair = jnp.einsum("rd,gfd->rgf", inputs, w_gate_up[0], preferred_element_type=jnp.float32)
    hidden = (jax.nn.silu(pair[:, 0]) * pair[:, 1]).astype(jnp.bfloat16)
    expert_terms = jnp.dot(hidden, w_down[0], preferred_element_type=jnp.float32).astype(
        jnp.bfloat16
    )
    results = lax.psum_scatter(expert_terms, "tp", scatter_dimension=1, tiled=True)
    returned = lax.all_to_all(
        results.reshape(ep_count, capacity, slice_width // 128, 128),
        "ep",
        split_axis=0,
        concat_axis=0,
        tiled=True,
    ).reshape(slot_rows, slice_width // 128, 128)
    return jnp.take(returned, jnp.maximum(place, 0), axis=0, mode="clip").astype(jnp.float32)


def body(
    attn_heads,
    w_out,
    resid_in,
    norm_gain,
    router_w,
    expert_ids,
    copy_pick,
    slot_expert,
    live_rows,
    w_gate_up,
    w_down,
):
    tp_count = lax.axis_size("tp")
    ep_count = lax.axis_size("ep")
    tp_index = lax.axis_index("tp")
    tok_rows, slice_width = resid_in.shape
    full_width = slice_width * tp_count
    top_count = expert_ids.shape[1]
    bound = max(2, 3 * tok_rows * top_count // (2 * (ep_count - ep_count // 16)))
    capacity = bound
    slot_rows = ep_count * capacity
    offset = tp_index * slice_width
    pair_tp = tp_count == 2

    heads = jnp.where(live_rows[0] > 0, attn_heads, jnp.zeros_like(attn_heads))
    proj = jnp.dot(heads, w_out, preferred_element_type=jnp.float32)
    resid_full = lax.dynamic_update_slice_in_dim(
        jnp.zeros((tok_rows, full_width), jnp.float32), resid_in.astype(jnp.float32), offset, 1
    )
    terms = proj + resid_full
    if pair_tp:
        total = terms + swap_tp(terms.astype(jnp.bfloat16)).astype(jnp.float32)
    else:
        total = lax.psum(terms, "tp")
    target = destinations(expert_ids, copy_pick, slot_expert)
    alive = jnp.arange(tok_rows, dtype=jnp.int32) < live_rows[0]

    target_kt = target.T
    alive_kt = jnp.broadcast_to(alive[None, :], target_kt.shape)
    flat_target = target_kt.reshape(-1)
    flat_alive = alive_kt.reshape(-1)
    slot_iota = jnp.arange(ep_count, dtype=jnp.int32)
    onehot = (flat_target[:, None] == slot_iota[None, :]) & flat_alive[:, None]
    choice_iota = jnp.arange(flat_target.shape[0], dtype=jnp.int32)
    lower = (choice_iota[:, None] >= choice_iota[None, :]).astype(jnp.bfloat16)
    counts = jnp.dot(lower, onehot.astype(jnp.bfloat16), preferred_element_type=jnp.float32)
    ranks = counts.astype(jnp.int32) - 1
    position = jnp.sum(jnp.where(onehot, ranks, 0), axis=1)

    ranks_early = position
    total, position = lax.optimization_barrier((total, position))
    stream_full = total.astype(jnp.bfloat16).astype(jnp.float32)
    mean_sq = jnp.mean(stream_full * stream_full, axis=1, keepdims=True)
    scale = lax.rsqrt(mean_sq + norm_eps)
    normed_full = (stream_full * scale * norm_gain.astype(jnp.float32)).astype(jnp.bfloat16)
    normed_part = lax.dynamic_slice_in_dim(normed_full, offset, slice_width, 1)
    stream_part = lax.dynamic_slice_in_dim(stream_full, offset, slice_width, 1)

    logits = jnp.dot(normed_full, router_w, preferred_element_type=jnp.float32)
    expert_iota = jnp.arange(router_w.shape[1], dtype=jnp.int32)
    chosen = jnp.sum(
        jnp.where(expert_ids[:, :, None] == expert_iota, logits[:, None, :], 0.0), axis=2
    )
    powers = jnp.exp(chosen)
    weights = powers / jnp.sum(powers, axis=1, keepdims=True)
    if pair_tp:
        fetched = rows_split_experts(
            flat_target, flat_alive, ranks_early, normed_full, w_gate_up, w_down, capacity, tp_index,
            total,
        )
    else:
        place = jnp.where(flat_alive, flat_target * capacity + position, -1)
        fetched = units_split_experts(
            place, normed_part, w_gate_up, w_down, capacity, tp_index
        )
    fetched = fetched.reshape(top_count, tok_rows, slice_width // 128, 128)
    scaled = (weights * alive[:, None].astype(jnp.float32)).T
    routed = jnp.sum(fetched * scaled[:, :, None, None], axis=0).reshape(tok_rows, slice_width)
    return (stream_part + routed).astype(jnp.bfloat16)


def solution(mesh):
    in_specs = (
        P("ep", "tp"),
        P("tp", None),
        P("ep", "tp"),
        P(),
        P(),
        P("ep", None),
        P("ep", None),
        P(),
        P("ep"),
        P("ep", None, "tp", None),
        P("ep", "tp", None),
    )
    out_specs = P("ep", "tp")
    return jax.shard_map(body, mesh=mesh, in_specs=in_specs, out_specs=out_specs, check_vma=False)
```
